128 devices in a mesh: slab: 32 (over y, x, core), img: 4 (over z).
Axes of the slice: x: 4, y: 4, z: 4, core: 2. Of those that a mesh axis runs over, the one named last changes fastest.
Arguments:
- volume: float32 [128, 1024, 1024], P('img', 'slab'), may hold values from -6 to 6
- blk_plane: int32 [512, 8], replicated, may hold values from 0 to 126, all different within a row; in each aligned block of 4 rows (0 to 3, 4 to 7, ...) at most 2 rows name the same one
- blk_row: int32 [512, 8], replicated, may hold values from 0 to 1022
- blk_col: int32 [512, 8], replicated, may hold values from 0 to 7
- frac_plane: float32 [512, 8], replicated, may hold values from 0 to 1
- frac_row: float32 [512, 8], replicated, may hold values from 0 to 1
- defocus: float32 [512], replicated, may hold values from 0.5 to 4
Outputs:
- slices: float32 [512, 8, 2, 128], P(('slab', 'img'))
The draws below stay inside these ranges and needn't reach their ends.
Inputs may be any that keep to these rules, and one draw needn't show every extreme that they name: `blk_plane`: the blocks of one image name different lower planes. Among the 4 images of one device (aligned groups of images), no plane is the lower plane of more than 2 blocks, and some plane reaches 2.
All inputs are finite; a program needn't handle non-finite values.
Results may differ from the reference program's by a relative error of at most 0.0003.
Values sent between devices are 32-bit elements; how exact they have to be, the bound alone decides.
No kernel may reach another device: no remote copies, remote signals or barrier semaphores. Data moves between devices by JAX's collectives and lax.ppermute only.
A program may use at most 128 MiB of HBM per device.

```python
import math
import jax
import jax.numpy as jnp
import numpy as np
from jax import lax

BOX = 1024
LANES = 128
IMG_DEV = 4
IMG_BLK = 8
MOST = 2
PLANES = 128
NIMG = 512


def touch_ends(array, stream_key, least, top_value):
    index_at = [jax.random.randint(jax.random.fold_in(stream_key, axis), (), 0, length) for axis, length in enumerate(array.shape)]
    main_axis = array.shape.index(max(array.shape))
    next_to = index_at[:main_axis] + [(index_at[main_axis] + 1) % array.shape[main_axis]] + index_at[main_axis + 1:]
    return array.at[tuple(index_at)].set(least).at[tuple(next_to)].set(top_value)


def steps_of(own_key, dims, pieces, smallest, largest):
    factor_of, own = 1.0, jax.random.fold_in(own_key, 6)
    for axis_at, blocks in pieces:
        draws = jnp.exp(jax.random.uniform(jax.random.fold_in(own, axis_at), (blocks,), jnp.float32, smallest / len(pieces), largest / len(pieces)))
        factor_of = factor_of * jnp.repeat(draws, dims[axis_at] // blocks).reshape([-1 if axis == axis_at else 1 for axis in range(len(dims))])
    return factor_of


def routed_block(stream_key, own, number, rows, number_of, top, reach, lean):
    sequence = jax.random.permutation(stream_key, number_of)
    crowded, usual = shares(number_of, rows * top, reach, lean, True), shares(number_of, rows * top, reach, lean, False)
    places = jnp.arange(number_of)

    def named(sizes, turn):
        used = int((sizes > 0).sum())
        fixed = max(1, used // 4)
        passed = fixed + (places - fixed + turn * (used - fixed)) % max(1, number_of - fixed)
        return jnp.zeros((number_of,), jnp.int32).at[sequence[jnp.where(places < fixed, places, passed)]].set(jnp.asarray(sizes, jnp.int32))

    sizes = jnp.where(number % 4 == 0, named(crowded, number // 4), named(usual, number - number // 4 - 1))
    mixed = jax.random.permutation(jax.random.fold_in(own, 3), number_of)
    giver, receiver = mixed[0:number_of // 2 * 2:2], mixed[1:number_of // 2 * 2:2]
    margin = jnp.minimum(sizes[giver] - 1, reach - sizes[receiver]) // 2
    margin = jnp.where((giver == sequence[0]) | (receiver == sequence[0]) | (sizes[receiver] == 0), 0, jnp.maximum(margin, 0))
    passed = jax.random.randint(jax.random.fold_in(own, 4), (number_of // 2,), 0, 1 << 20) % (margin + 1)
    sizes = sizes.at[giver].add(-passed).at[receiver].add(passed)
    labels = jnp.searchsorted(jnp.cumsum(sizes), jnp.arange(rows * top), side="right").astype(jnp.int32)
    grid = labels.reshape(top, rows).T
    grid = grid[jax.random.permutation(jax.random.fold_in(own, 1), rows)]
    turn = jax.random.randint(jax.random.fold_in(own, 2), (rows, 1), 0, top)
    return jnp.take_along_axis(grid, (jnp.arange(top)[None, :] + turn) % top, axis=1)


def shares(number_of, total, most, skew, full):
    loads = [(1 << 20) // math.isqrt(grade ** skew) + 1 for grade in range(1, number_of + 1)]
    largest = most if full else min(most, max(-(-total // number_of), total * loads[0] // sum(loads)))
    least = 1 if total - largest >= number_of - 1 else 0
    counts, spare = [largest] + [least] * (number_of - 1), total - largest - least * (number_of - 1)
    while spare > 0:
        free = [i for i in range(1, number_of) if counts[i] < largest] or [i for i in range(1, number_of) if counts[i] < most]
        pool, left = sum([loads[i] for i in free]), spare
        for i in free:
            more = min(most - counts[i], max(1, left * loads[i] // pool), spare)
            counts[i] = counts[i] + more
            spare = spare - more
    return np.array(counts)


def scatter_about(rng, shape, deviation, limit, split=(), held_as=jnp.bfloat16):
    values = deviation * jax.random.normal(rng, shape, jnp.float32)
    if split:
        values = values * steps_of(rng, shape, split, -0.22, 0.18)
    return jnp.clip(values, -limit, limit).astype(held_as)


def setup_inputs(seed: int = 0) -> dict:
    key_of = jax.random.split(jax.random.key(seed), 8)
    volume = scatter_about(key_of[0], (PLANES, BOX, BOX), 1.0, 6.0, ((0, 4), (1, 32)), jnp.float32)
    blk_plane_keys = jax.random.split(jax.random.fold_in(key_of[1], 1), NIMG // IMG_DEV)
    blk_plane_turns = jax.random.permutation(jax.random.fold_in(key_of[1], 3), NIMG // IMG_DEV)
    blk_plane = jax.vmap(lambda own, number: routed_block(jax.random.fold_in(key_of[1], 2), own, number, IMG_DEV, PLANES - 1, IMG_BLK, MOST, 2))(blk_plane_keys, blk_plane_turns).reshape((NIMG, IMG_BLK))
    blk_row = touch_ends(jax.random.randint(key_of[2], (NIMG, IMG_BLK), 0, BOX - 1), jax.random.fold_in(key_of[2], 1), 0, (BOX - 1) - 1).astype(jnp.int32)
    blk_col = touch_ends(jax.random.randint(key_of[3], (NIMG, IMG_BLK), 0, BOX // LANES), jax.random.fold_in(key_of[3], 1), 0, (BOX // LANES) - 1).astype(jnp.int32)
    frac_plane = jnp.clip(jax.random.uniform(key_of[4], (NIMG, IMG_BLK), jnp.float32, 0.0, 1.0), 0.0, 1.0)
    frac_row = jnp.clip(jax.random.uniform(key_of[5], (NIMG, IMG_BLK), jnp.float32, 0.0, 1.0), 0.0, 1.0)
    defocus = jnp.clip(jnp.exp(jax.random.uniform(key_of[6], (NIMG,), jnp.float32, math.log(0.5), math.log(4.0))), 0.5, 4.0)
    return {"volume": volume, "blk_plane": blk_plane, "blk_row": blk_row, "blk_col": blk_col, "frac_plane": frac_plane, "frac_row": frac_row, "defocus": defocus}


CTF_SCALE = 20.0
CTF_PHASE = 0.07


def reference(volume, blk_plane, blk_row, blk_col, frac_plane, frac_row, defocus):
    plane_idx = blk_plane.reshape(-1).astype(jnp.int32)
    rows = blk_row.reshape(-1).astype(jnp.int32)
    cols = blk_col.reshape(-1).astype(jnp.int32)
    frac_z = frac_plane.reshape(-1)
    frac_y = frac_row.reshape(-1)[:, None]
    focus = jnp.repeat(defocus, IMG_BLK)
    lane = jnp.arange(LANES, dtype=jnp.int32)
    column_x = cols[:, None] * LANES + lane[None, :]
    fold_x = jnp.minimum(column_x, BOX - column_x).astype(jnp.float32)
    fold_y = jnp.minimum(rows, BOX - rows).astype(jnp.float32)
    wave_sq = (fold_x * fold_x + (fold_y * fold_y)[:, None]) / float(BOX * BOX)
    ctf_value = -jnp.sin(CTF_SCALE * focus[:, None] * wave_sq + CTF_PHASE)
    per_row = BOX // LANES
    index_low = rows * per_row + cols
    index_high = index_low + per_row

    def step(carry, item):
        plane, here = item
        spectrum = jnp.fft.fft2(plane, norm="ortho")
        flat_real = jnp.real(spectrum).reshape(-1, LANES)
        flat_imag = jnp.imag(spectrum).reshape(-1, LANES)
        weight = jnp.where(plane_idx == here, 1.0 - frac_z, 0.0) + jnp.where(plane_idx + 1 == here, frac_z, 0.0)
        scale = weight[:, None] * ctf_value
        part_real = scale * ((1.0 - frac_y) * flat_real[index_low] + frac_y * flat_real[index_high])
        part_imag = scale * ((1.0 - frac_y) * flat_imag[index_low] + frac_y * flat_imag[index_high])
        return (carry[0] + part_real, carry[1] + part_imag), None

    empty = jnp.zeros((plane_idx.shape[0], LANES), jnp.float32)
    (total_real, total_imag), _ = lax.scan(step, (empty, empty), (volume, jnp.arange(PLANES, dtype=jnp.int32)))
    stacked = jnp.stack([total_real, total_imag], axis=1)
    return stacked.reshape(NIMG, IMG_BLK, 2, LANES)
```

```python
import math

import jax
import jax.numpy as jnp
from jax import lax
from jax.sharding import PartitionSpec as P

LANES = 128


CTF_SCALE = 20.0
CTF_PHASE = 0.07
HIGH = lax.Precision.HIGHEST


def dft_tables(length):
    steps = lax.iota(jnp.int32, length)
    phase = steps[:, None] * steps[None, :] % length
    angle = phase.astype(jnp.float32) * (2.0 * math.pi / length)
    factor = 1.0 / math.sqrt(length)
    return (jnp.cos(angle) * factor, jnp.sin(angle) * factor)


def column_transform(field, cosine, sine):
    real_part = jnp.einsum("prx,xk->prk", field, cosine, precision=HIGH)
    imag_part = -jnp.einsum("prx,xk->prk", field, sine, precision=HIGH)
    return (real_part, imag_part)


def row_transform(pieces, cosine, sine):
    real_part, imag_part = pieces
    out_real = jnp.einsum("kr,prc->pkc", cosine, real_part, precision=HIGH) + jnp.einsum(
        "kr,prc->pkc", sine, imag_part, precision=HIGH
    )
    out_imag = jnp.einsum("kr,prc->pkc", cosine, imag_part, precision=HIGH) - jnp.einsum(
        "kr,prc->pkc", sine, real_part, precision=HIGH
    )
    return (out_real, out_imag)


def slot_tables(blk_plane, n_dev):
    plane = blk_plane.reshape(n_dev, -1)
    k_dev = plane.shape[1]
    order = lax.iota(jnp.int32, k_dev)
    same = plane[:, :, None] == plane[:, None, :]
    earlier = order[None, None, :] < order[None, :, None]
    rank = jnp.sum((same & earlier).astype(jnp.int32), axis=2)
    return plane, rank


def send_parts(plane_real, plane_imag, first_plane, meta, box, n_dev):
    blk_plane, blk_row, blk_col, frac_plane, frac_row, defocus = meta
    n_blk = blk_plane.shape[1]
    plane, rank = slot_tables(blk_plane, n_dev)
    k_dev = plane.shape[1]
    own = plane_real.shape[0]
    t = lax.iota(jnp.int32, own)[:, None, None]
    side = lax.iota(jnp.int32, 2)[None, :, None]
    u = lax.iota(jnp.int32, 2)[None, None, :]
    target = first_plane + t - side
    match = (plane[:, None, None, None, :] == target[None, :, :, :, None]) & (
        rank[:, None, None, None, :] == u[None, :, :, :, None]
    )
    valid = jnp.any(match, axis=-1)
    kidx = jnp.sum(jnp.where(match, lax.iota(jnp.int32, k_dev), 0), axis=-1)
    g = lax.iota(jnp.int32, n_dev)[:, None, None, None] * k_dev + kidx
    g = g.reshape(-1)
    rows = blk_row.reshape(-1)[g]
    cols = blk_col.reshape(-1)[g]
    frac_z = frac_plane.reshape(-1)[g]
    frac_y = frac_row.reshape(-1)[g][:, None]
    focus = defocus[g // n_blk]
    side_f = jnp.broadcast_to(side, (n_dev, own, 2, 2)).reshape(-1)
    valid = valid.reshape(-1)
    t_idx = jnp.broadcast_to(t, (n_dev, own, 2, 2)).reshape(-1)
    lane = lax.iota(jnp.int32, LANES)
    column_x = cols[:, None] * LANES + lane[None, :]
    fold_x = jnp.minimum(column_x, box - column_x).astype(jnp.float32)
    fold_y = jnp.minimum(rows, box - rows).astype(jnp.float32)
    wave_sq = (fold_x * fold_x + (fold_y * fold_y)[:, None]) / float(box * box)
    ctf_value = -jnp.sin(CTF_SCALE * focus[:, None] * wave_sq + CTF_PHASE)
    per_row = box // LANES
    index_low = t_idx * (box * per_row) + rows * per_row + cols
    index_high = index_low + per_row
    weight = jnp.where(side_f == 0, 1.0 - frac_z, frac_z)
    weight = jnp.where(valid, weight, 0.0)
    scale = weight[:, None] * ctf_value
    flat_real = plane_real.reshape(-1, LANES)
    flat_imag = plane_imag.reshape(-1, LANES)
    part_real = scale * ((1.0 - frac_y) * flat_real[index_low] + frac_y * flat_real[index_high])
    part_imag = scale * ((1.0 - frac_y) * flat_imag[index_low] + frac_y * flat_imag[index_high])
    parts = jnp.stack([part_real, part_imag], axis=1)
    return parts.reshape(n_dev, own * 4, 2, LANES)


def gather_parts(recv, blk_plane, me, own, n_slab, n_img):
    n_dev = n_slab * n_img
    plane, rank = slot_tables(blk_plane, n_dev)
    mine = plane[me]
    my_rank = rank[me]
    slots = own * 4

    def place(q, side):
        holder = q // own
        src = (holder % n_slab) * n_img + holder // n_slab
        return src * slots + (q % own) * 4 + side * 2 + my_rank

    flat = recv.reshape(-1, 2, LANES)
    return flat[place(mine, 0)] + flat[place(mine + 1, 1)]


def on_device(volume, blk_plane, blk_row, blk_col, frac_plane, frac_row, defocus):
    box = volume.shape[2]
    cosine, sine = dft_tables(box)
    n_slab = lax.axis_size("slab")
    n_img = lax.axis_size("img")
    n_dev = n_slab * n_img
    col_real, col_imag = column_transform(volume, cosine, sine)
    plane_real, plane_imag = row_transform(
        (
            lax.all_to_all(col_real, "slab", split_axis=0, concat_axis=1, tiled=True),
            lax.all_to_all(col_imag, "slab", split_axis=0, concat_axis=1, tiled=True),
        ),
        cosine,
        sine,
    )
    own = plane_real.shape[0]
    first_plane = (lax.axis_index("img") * n_slab + lax.axis_index("slab")) * own
    meta = (blk_plane, blk_row, blk_col, frac_plane, frac_row, defocus)
    parts = send_parts(plane_real, plane_imag, first_plane, meta, box, n_dev)
    recv = lax.all_to_all(parts, ("slab", "img"), split_axis=0, concat_axis=0, tiled=True)
    me = lax.axis_index("slab") * n_img + lax.axis_index("img")
    total = gather_parts(recv, blk_plane, me, own, n_slab, n_img)
    n_blk = blk_plane.shape[1]
    return total.reshape(-1, n_blk, 2, LANES)


def solution(mesh):
    placed = (P("img", "slab", None), P(), P(), P(), P(), P(), P())
    return jax.shard_map(
        on_device,
        mesh=mesh,
        in_specs=placed,
        out_specs=P(("slab", "img"), None, None, None),
        check_vma=False,
    )
```

```python
import math

import jax
import jax.numpy as jnp
from jax import lax
from jax.sharding import PartitionSpec as P

LANES = 128
SPLIT = 8


CTF_SCALE = 20.0
CTF_PHASE = 0.07
HIGH = lax.Precision.HIGHEST


def roots(rows, cols, length, factor):
    phase = rows * cols % length
    angle = phase.astype(jnp.float32) * (2.0 * math.pi / length)
    return (jnp.cos(angle) * factor, -jnp.sin(angle) * factor)


def small_dft(length):
    re, im = [], []
    for k in range(length):
        re.append([round(math.cos(2 * math.pi * k * n / length), 15) for n in range(length)])
        im.append([round(-math.sin(2 * math.pi * k * n / length), 15) for n in range(length)])
    return re, im


def combine(coef, pieces):
    total = None
    for c, piece in zip(coef, pieces):
        if c == 0.0:
            continue
        term = piece if c == 1.0 else (-piece if c == -1.0 else c * piece)
        total = term if total is None else total + term
    return total


def row_fft(plane):
    own, n, x = plane.shape
    m = n // SPLIT
    c8, s8 = small_dft(SPLIT)
    slabs = [plane[:, j * m:(j + 1) * m, :] for j in range(SPLIT)]
    a_re = jnp.stack([combine(c8[k], slabs) for k in range(SPLIT)], axis=1)
    a_im = jnp.stack(
        [combine(s8[k], slabs) if k != 0 else jnp.zeros_like(slabs[0]) for k in range(SPLIT)],
        axis=1,
    )
    k1 = lax.iota(jnp.int32, SPLIT)[:, None]
    n2 = lax.iota(jnp.int32, m)[None, :]
    t_re, t_im = roots(k1, n2, n, 1.0)
    t_re = t_re[None, :, :, None]
    t_im = t_im[None, :, :, None]
    b_re = a_re * t_re - a_im * t_im
    b_im = a_re * t_im + a_im * t_re
    idx = lax.iota(jnp.int32, m)
    w_re, w_im = roots(idx[:, None], idx[None, :], m, 1.0 / math.sqrt(n))
    mm = lambda w, b: jnp.einsum("kn,pjnc->pjkc", w, b, precision=HIGH)
    v_re = mm(w_re, b_re) - mm(w_im, b_im)
    v_im = mm(w_re, b_im) + mm(w_im, b_re)
    return v_re.reshape(own * n, x), v_im.reshape(own * n, x)


def column_fft_block(r_re, r_im, cols, box):
    s, x = r_re.shape
    m = x // SPLIT
    t_re = jnp.swapaxes(r_re.reshape(s, m, SPLIT), 1, 2)
    t_im = jnp.swapaxes(r_im.reshape(s, m, SPLIT), 1, 2)
    idx = lax.iota(jnp.int32, m)
    w_re, w_im = roots(idx[:, None], idx[None, :], m, 1.0 / math.sqrt(x))
    mm = lambda a, w: jnp.einsum("sjn,nl->sjl", a, w, precision=HIGH)
    y_re = mm(t_re, w_re) - mm(t_im, w_im)
    y_im = mm(t_re, w_im) + mm(t_im, w_re)
    n1 = lax.iota(jnp.int32, SPLIT)
    lane = lax.iota(jnp.int32, LANES)
    column_x = cols[:, None, None] * LANES + lane[None, None, :]
    g_re, g_im = roots(n1[None, :, None], column_x, box, 1.0)
    out_re = jnp.sum(g_re * y_re - g_im * y_im, axis=1)
    out_im = jnp.sum(g_re * y_im + g_im * y_re, axis=1)
    return out_re, out_im


def slot_tables(blk_plane, n_dev):
    plane = blk_plane.reshape(n_dev, -1)
    k_dev = plane.shape[1]
    order = lax.iota(jnp.int32, k_dev)
    same = plane[:, :, None] == plane[:, None, :]
    earlier = order[None, None, :] < order[None, :, None]
    rank = jnp.sum((same & earlier).astype(jnp.int32), axis=2)
    return plane, rank


def send_parts(v_re, v_im, first_plane, own, meta, box, n_dev):
    blk_plane, blk_row, blk_col, frac_plane, frac_row, defocus = meta
    n_blk = blk_plane.shape[1]
    plane, rank = slot_tables(blk_plane, n_dev)
    k_dev = plane.shape[1]
    t = lax.iota(jnp.int32, own)[:, None, None]
    side = lax.iota(jnp.int32, 2)[None, :, None]
    u = lax.iota(jnp.int32, 2)[None, None, :]
    target = first_plane + t - side
    match = (plane[:, None, None, None, :] == target[None, :, :, :, None]) & (
        rank[:, None, None, None, :] == u[None, :, :, :, None]
    )
    valid = jnp.any(match, axis=-1)
    kidx = jnp.sum(jnp.where(match, lax.iota(jnp.int32, k_dev), 0), axis=-1)
    g = lax.iota(jnp.int32, n_dev)[:, None, None, None] * k_dev + kidx
    g = g.reshape(-1)
    rows = blk_row.reshape(-1)[g]
    cols = blk_col.reshape(-1)[g]
    frac_z = frac_plane.reshape(-1)[g]
    frac_y = frac_row.reshape(-1)[g][:, None]
    focus = defocus[g // n_blk]
    side_f = jnp.broadcast_to(side, (n_dev, own, 2, 2)).reshape(-1)
    valid = valid.reshape(-1)
    t_idx = jnp.broadcast_to(t, (n_dev, own, 2, 2)).reshape(-1)
    lane = lax.iota(jnp.int32, LANES)
    column_x = cols[:, None] * LANES + lane[None, :]
    fold_x = jnp.minimum(column_x, box - column_x).astype(jnp.float32)
    fold_y = jnp.minimum(rows, box - rows).astype(jnp.float32)
    wave_sq = (fold_x * fold_x + (fold_y * fold_y)[:, None]) / float(box * box)
    ctf_value = -jnp.sin(CTF_SCALE * focus[:, None] * wave_sq + CTF_PHASE)
    m = box // SPLIT

    def stored(r):
        return t_idx * box + (r % SPLIT) * m + r // SPLIT

    index_low = stored(rows)
    index_high = stored(rows + 1)
    weight = jnp.where(side_f == 0, 1.0 - frac_z, frac_z)
    weight = jnp.where(valid, weight, 0.0)
    scale = weight[:, None] * ctf_value
    r_re = (1.0 - frac_y) * v_re[index_low] + frac_y * v_re[index_high]
    r_im = (1.0 - frac_y) * v_im[index_low] + frac_y * v_im[index_high]
    o_re, o_im = column_fft_block(r_re, r_im, cols, box)
    parts = jnp.stack([scale * o_re, scale * o_im], axis=1)
    return parts.reshape(n_dev, own * 4, 2, LANES)


def gather_parts(recv, blk_plane, me, own, n_slab, n_img):
    n_dev = n_slab * n_img
    plane, rank = slot_tables(blk_plane, n_dev)
    mine = plane[me]
    my_rank = rank[me]
    slots = own * 4

    def place(q, side):
        holder = q // own
        src = (holder % n_slab) * n_img + holder // n_slab
        return src * slots + (q % own) * 4 + side * 2 + my_rank

    flat = recv.reshape(-1, 2, LANES)
    return flat[place(mine, 0)] + flat[place(mine + 1, 1)]


def on_device(volume, blk_plane, blk_row, blk_col, frac_plane, frac_row, defocus):
    box = volume.shape[2]
    n_slab = lax.axis_size("slab")
    n_img = lax.axis_size("img")
    n_dev = n_slab * n_img
    plane = lax.all_to_all(volume, "slab", split_axis=0, concat_axis=1, tiled=True)
    own = plane.shape[0]
    v_re, v_im = row_fft(plane)
    first_plane = (lax.axis_index("img") * n_slab + lax.axis_index("slab")) * own
    meta = (blk_plane, blk_row, blk_col, frac_plane, frac_row, defocus)
    parts = send_parts(v_re, v_im, first_plane, own, meta, box, n_dev)
    recv = lax.all_to_all(parts, ("slab", "img"), split_axis=0, concat_axis=0, tiled=True)
    me = lax.axis_index("slab") * n_img + lax.axis_index("img")
    total = gather_parts(recv, blk_plane, me, own, n_slab, n_img)
    n_blk = blk_plane.shape[1]
    return total.reshape(-1, n_blk, 2, LANES)


def solution(mesh):
    placed = (P("img", "slab", None), P(), P(), P(), P(), P(), P())
    return jax.shard_map(
        on_device,
        mesh=mesh,
        in_specs=placed,
        out_specs=P(("slab", "img"), None, None, None),
        check_vma=False,
    )
```

```python
import math

import jax
import jax.numpy as jnp
from jax import lax
from jax.sharding import PartitionSpec as P

LANES = 128
SPLIT = 8


CTF_SCALE = 20.0
CTF_PHASE = 0.07
MID = lax.Precision.HIGH


def roots(rows, cols, length, factor):
    phase = rows * cols % length
    angle = phase.astype(jnp.float32) * (2.0 * math.pi / length)
    return (jnp.cos(angle) * factor, -jnp.sin(angle) * factor)


def slot_tables(blk_plane, n_dev):
    plane = blk_plane.reshape(n_dev, -1)
    k_dev = plane.shape[1]
    order = lax.iota(jnp.int32, k_dev)
    same = plane[:, :, None] == plane[:, None, :]
    earlier = order[None, None, :] < order[None, :, None]
    rank = jnp.sum((same & earlier).astype(jnp.int32), axis=2)
    return plane, rank


def send_parts(plane, first_plane, meta, box, n_dev):
    blk_plane, blk_row, blk_col, frac_plane, frac_row, defocus = meta
    n_blk = blk_plane.shape[1]
    own, n_rows, x = plane.shape
    plane_of, rank = slot_tables(blk_plane, n_dev)
    k_dev = plane_of.shape[1]
    t = lax.iota(jnp.int32, own)[:, None, None, None]
    side = lax.iota(jnp.int32, 2)[None, None, :, None]
    u = lax.iota(jnp.int32, 2)[None, None, None, :]
    target = first_plane + t - side
    match = (plane_of[None, :, None, None, :] == target[..., None]) & (
        rank[None, :, None, None, :] == u[..., None]
    )
    valid = jnp.any(match, axis=-1)
    kidx = jnp.sum(jnp.where(match, lax.iota(jnp.int32, k_dev), 0), axis=-1)
    g = lax.iota(jnp.int32, n_dev)[None, :, None, None] * k_dev + kidx
    g = g.reshape(-1)
    rows = blk_row.reshape(-1)[g]
    cols = blk_col.reshape(-1)[g]
    frac_z = frac_plane.reshape(-1)[g]
    frac_y = frac_row.reshape(-1)[g][:, None]
    focus = defocus[g // n_blk]
    side_f = jnp.broadcast_to(side, (own, n_dev, 2, 2)).reshape(-1)
    valid = valid.reshape(-1)
    lane = lax.iota(jnp.int32, LANES)
    column_x = cols[:, None] * LANES + lane[None, :]
    fold_x = jnp.minimum(column_x, box - column_x).astype(jnp.float32)
    fold_y = jnp.minimum(rows, box - rows).astype(jnp.float32)
    wave_sq = (fold_x * fold_x + (fold_y * fold_y)[:, None]) / float(box * box)
    ctf_value = -jnp.sin(CTF_SCALE * focus[:, None] * wave_sq + CTF_PHASE)
    weight = jnp.where(side_f == 0, 1.0 - frac_z, frac_z)
    weight = jnp.where(valid, weight, 0.0)
    scale = weight[:, None] * ctf_value
    step = int(math.isqrt(n_rows))
    a = lax.iota(jnp.int32, n_rows // step)[None, :]
    b = lax.iota(jnp.int32, step)[None, :]

    def row_roots(r):
        a_re, a_im = roots(r[:, None], a * step, n_rows, 1.0)
        b_re, b_im = roots(r[:, None], b, n_rows, 1.0)
        w_re = a_re[:, :, None] * b_re[:, None, :] - a_im[:, :, None] * b_im[:, None, :]
        w_im = a_re[:, :, None] * b_im[:, None, :] + a_im[:, :, None] * b_re[:, None, :]
        return w_re.reshape(-1, n_rows), w_im.reshape(-1, n_rows)

    lo_re, lo_im = row_roots(rows)
    hi_re, hi_im = row_roots(rows + 1)
    norm = 1.0 / math.sqrt(n_rows)
    w_re = ((1.0 - frac_y) * lo_re + frac_y * hi_re) * norm
    w_im = ((1.0 - frac_y) * lo_im + frac_y * hi_im) * norm
    n_s = w_re.shape[0] // own
    w_all = jnp.stack([w_re.reshape(own, n_s, n_rows), w_im.reshape(own, n_s, n_rows)], axis=1)
    r_all = jnp.einsum("tpsr,trc->tpsc", w_all, plane, precision=MID)
    m = x // SPLIT
    r4 = r_all.reshape(own, 2, n_s, SPLIT, m)
    idx = lax.iota(jnp.int32, m)
    c_re, c_im = roots(idx[:, None], idx[None, :], m, 1.0 / math.sqrt(x))
    w_col = jnp.stack(
        [jnp.concatenate([c_re, c_im], axis=1), jnp.concatenate([-c_im, c_re], axis=1)], axis=0
    )
    y = jnp.einsum("tpsjn,pnl->tsjl", r4, w_col, precision=MID).reshape(own * n_s, SPLIT, 2 * m)
    y_re = y[:, :, :m]
    y_im = y[:, :, m:]
    n1 = lax.iota(jnp.int32, SPLIT)
    e_re, e_im = roots(cols[:, None], n1[None, :], SPLIT, 1.0)
    t_re, t_im = roots(n1[:, None], lane[None, :], box, 1.0)
    g_re = e_re[:, :, None] * t_re[None] - e_im[:, :, None] * t_im[None]
    g_im = e_re[:, :, None] * t_im[None] + e_im[:, :, None] * t_re[None]
    o_re = jnp.sum(g_re * y_re - g_im * y_im, axis=1)
    o_im = jnp.sum(g_re * y_im + g_im * y_re, axis=1)
    parts = jnp.stack([scale * o_re, scale * o_im], axis=1)
    parts = parts.reshape(own, n_dev, 4, 2, LANES)
    return jnp.swapaxes(parts, 0, 1).reshape(n_dev, own * 4, 2, LANES)


def gather_parts(recv, blk_plane, me, own, n_slab, n_img):
    n_dev = n_slab * n_img
    plane, rank = slot_tables(blk_plane, n_dev)
    mine = plane[me]
    my_rank = rank[me]
    slots = own * 4

    def place(q, side):
        holder = q // own
        src = (holder % n_slab) * n_img + holder // n_slab
        return src * slots + (q % own) * 4 + side * 2 + my_rank

    flat = recv.reshape(-1, 2, LANES)
    return flat[place(mine, 0)] + flat[place(mine + 1, 1)]


def on_device(volume, blk_plane, blk_row, blk_col, frac_plane, frac_row, defocus):
    box = volume.shape[2]
    n_slab = lax.axis_size("slab")
    n_img = lax.axis_size("img")
    n_dev = n_slab * n_img
    p_loc, r_loc, x = volume.shape
    spread = jnp.swapaxes(volume.reshape(p_loc, r_loc, x // SPLIT, SPLIT), 2, 3)
    spread = spread.reshape(p_loc, r_loc, x)
    plane = lax.all_to_all(spread, "slab", split_axis=0, concat_axis=1, tiled=True)
    own = plane.shape[0]
    first_plane = (lax.axis_index("img") * n_slab + lax.axis_index("slab")) * own
    meta = (blk_plane, blk_row, blk_col, frac_plane, frac_row, defocus)
    parts = send_parts(plane, first_plane, meta, box, n_dev)
    recv = lax.all_to_all(parts, ("slab", "img"), split_axis=0, concat_axis=0, tiled=True)
    me = lax.axis_index("slab") * n_img + lax.axis_index("img")
    total = gather_parts(recv, blk_plane, me, own, n_slab, n_img)
    n_blk = blk_plane.shape[1]
    return total.reshape(-1, n_blk, 2, LANES)


def solution(mesh):
    placed = (P("img", "slab", None), P(), P(), P(), P(), P(), P())
    return jax.shard_map(
        on_device,
        mesh=mesh,
        in_specs=placed,
        out_specs=P(("slab", "img"), None, None, None),
        check_vma=False,
    )
```

```python
import math

import jax
import jax.numpy as jnp
from jax import lax
from jax.sharding import PartitionSpec as P

LANES = 128
SPLIT = 8


CTF_SCALE = 20.0
CTF_PHASE = 0.07
MID = lax.Precision.HIGH


def roots(rows, cols, length, factor):
    phase = rows * cols % length
    angle = phase.astype(jnp.float32) * (2.0 * math.pi / length)
    return (jnp.cos(angle) * factor, -jnp.sin(angle) * factor)


def slot_tables(blk_plane, n_dev):
    plane = blk_plane.reshape(n_dev, -1)
    k_dev = plane.shape[1]
    order = lax.iota(jnp.int32, k_dev)
    same = plane[:, :, None] == plane[:, None, :]
    earlier = order[None, None, :] < order[None, :, None]
    rank = jnp.sum((same & earlier).astype(jnp.int32), axis=2)
    return plane, rank


def send_parts(plane, first_plane, meta, box, n_dev):
    blk_plane, blk_row, blk_col, frac_plane, frac_row, defocus = meta
    n_blk = blk_plane.shape[1]
    own, n_rows, x = plane.shape
    plane_of, rank = slot_tables(blk_plane, n_dev)
    k_dev = plane_of.shape[1]
    t = lax.iota(jnp.int32, own)[:, None, None, None]
    side = lax.iota(jnp.int32, 2)[None, None, :, None]
    u = lax.iota(jnp.int32, 2)[None, None, None, :]
    target = first_plane + t - side
    match = (plane_of[None, :, None, None, :] == target[..., None]) & (
        rank[None, :, None, None, :] == u[..., None]
    )
    valid = jnp.any(match, axis=-1)
    kidx = jnp.sum(jnp.where(match, lax.iota(jnp.int32, k_dev), 0), axis=-1)
    g = lax.iota(jnp.int32, n_dev)[None, :, None, None] * k_dev + kidx
    g = g.reshape(-1)
    rows = blk_row.reshape(-1)[g]
    cols = blk_col.reshape(-1)[g]
    frac_z = frac_plane.reshape(-1)[g]
    frac_y = frac_row.reshape(-1)[g][:, None]
    focus = defocus[g // n_blk]
    side_f = jnp.broadcast_to(side, (own, n_dev, 2, 2)).reshape(-1)
    valid = valid.reshape(-1)
    lane = lax.iota(jnp.int32, LANES)
    column_x = cols[:, None] * LANES + lane[None, :]
    fold_x = jnp.minimum(column_x, box - column_x).astype(jnp.float32)
    fold_y = jnp.minimum(rows, box - rows).astype(jnp.float32)
    wave_sq = (fold_x * fold_x + (fold_y * fold_y)[:, None]) / float(box * box)
    ctf_value = -jnp.sin(CTF_SCALE * focus[:, None] * wave_sq + CTF_PHASE)
    weight = jnp.where(side_f == 0, 1.0 - frac_z, frac_z)
    weight = jnp.where(valid, weight, 0.0)
    scale = weight[:, None] * ctf_value
    step = int(math.isqrt(n_rows))
    a = lax.iota(jnp.int32, n_rows // step)[None, :]
    b = lax.iota(jnp.int32, step)[None, :]

    def row_roots(r):
        a_re, a_im = roots(r[:, None], a * step, n_rows, 1.0)
        b_re, b_im = roots(r[:, None], b, n_rows, 1.0)
        w_re = a_re[:, :, None] * b_re[:, None, :] - a_im[:, :, None] * b_im[:, None, :]
        w_im = a_re[:, :, None] * b_im[:, None, :] + a_im[:, :, None] * b_re[:, None, :]
        return w_re.reshape(-1, n_rows), w_im.reshape(-1, n_rows)

    lo_re, lo_im = row_roots(rows)
    hi_re, hi_im = row_roots(rows + 1)
    norm = 1.0 / math.sqrt(n_rows)
    w_re = ((1.0 - frac_y) * lo_re + frac_y * hi_re) * norm
    w_im = ((1.0 - frac_y) * lo_im + frac_y * hi_im) * norm
    n_s = w_re.shape[0] // own
    w_all = jnp.stack([w_re.reshape(own, n_s, n_rows), w_im.reshape(own, n_s, n_rows)], axis=1)
    r_t = jnp.einsum("trc,tpsr->tpcs", plane, w_all, precision=MID)
    m = x // SPLIT
    r5 = r_t.reshape(own, 2, m, SPLIT, n_s)
    idx = lax.iota(jnp.int32, m)
    c_re, c_im = roots(idx[:, None], idx[None, :], m, 1.0 / math.sqrt(x))
    w_col = jnp.stack(
        [jnp.stack([c_re, -c_im], axis=1), jnp.stack([c_im, c_re], axis=1)], axis=0
    )
    y = jnp.einsum("qkpn,tpnjs->tqkjs", w_col, r5, precision=MID)
    y_re = y[:, 0]
    y_im = y[:, 1]
    n1 = lax.iota(jnp.int32, SPLIT)
    cols_t = cols.reshape(own, n_s)
    e_re, e_im = roots(n1[None, :, None], cols_t[:, None, :], SPLIT, 1.0)
    t_re, t_im = roots(lane[:, None], n1[None, :], box, 1.0)
    e_re = e_re[:, None]
    e_im = e_im[:, None]
    t_re = t_re[None, :, :, None]
    t_im = t_im[None, :, :, None]
    g_re = e_re * t_re - e_im * t_im
    g_im = e_re * t_im + e_im * t_re
    o_re = jnp.sum(g_re * y_re - g_im * y_im, axis=2)
    o_im = jnp.sum(g_re * y_im + g_im * y_re, axis=2)
    o_re = jnp.swapaxes(o_re, 1, 2).reshape(own * n_s, LANES)
    o_im = jnp.swapaxes(o_im, 1, 2).reshape(own * n_s, LANES)
    parts = jnp.stack([scale * o_re, scale * o_im], axis=1)
    parts = parts.reshape(own, n_dev, 4, 2, LANES)
    return jnp.swapaxes(parts, 0, 1).reshape(n_dev, own * 4, 2, LANES)


def gather_parts(recv, blk_plane, me, own, n_slab, n_img):
    n_dev = n_slab * n_img
    plane, rank = slot_tables(blk_plane, n_dev)
    mine = plane[me]
    my_rank = rank[me]
    slots = own * 4

    def place(q, side):
        holder = q // own
        src = (holder % n_slab) * n_img + holder // n_slab
        return src * slots + (q % own) * 4 + side * 2 + my_rank

    flat = recv.reshape(-1, 2, LANES)
    return flat[place(mine, 0)] + flat[place(mine + 1, 1)]


def on_device(volume, blk_plane, blk_row, blk_col, frac_plane, frac_row, defocus):
    box = volume.shape[2]
    n_slab = lax.axis_size("slab")
    n_img = lax.axis_size("img")
    n_dev = n_slab * n_img
    plane = lax.all_to_all(volume, "slab", split_axis=0, concat_axis=1, tiled=True)
    own = plane.shape[0]
    first_plane = (lax.axis_index("img") * n_slab + lax.axis_index("slab")) * own
    meta = (blk_plane, blk_row, blk_col, frac_plane, frac_row, defocus)
    parts = send_parts(plane, first_plane, meta, box, n_dev)
    recv = lax.all_to_all(parts, ("slab", "img"), split_axis=0, concat_axis=0, tiled=True)
    me = lax.axis_index("slab") * n_img + lax.axis_index("img")
    total = gather_parts(recv, blk_plane, me, own, n_slab, n_img)
    n_blk = blk_plane.shape[1]
    return total.reshape(-1, n_blk, 2, LANES)


def solution(mesh):
    placed = (P("img", "slab", None), P(), P(), P(), P(), P(), P())
    return jax.shard_map(
        on_device,
        mesh=mesh,
        in_specs=placed,
        out_specs=P(("slab", "img"), None, None, None),
        check_vma=False,
    )
```

```python
import math

import jax
import jax.numpy as jnp
from jax import lax
from jax.sharding import PartitionSpec as P

LANES = 128
SPLIT = 8


CTF_SCALE = 20.0
CTF_PHASE = 0.07
MID = lax.Precision.HIGH


def roots(rows, cols, length, factor):
    phase = rows * cols % length
    angle = phase.astype(jnp.float32) * (2.0 * math.pi / length)
    return (jnp.cos(angle) * factor, -jnp.sin(angle) * factor)


def slot_tables(blk_plane, n_dev):
    plane = blk_plane.reshape(n_dev, -1)
    k_dev = plane.shape[1]
    order = lax.iota(jnp.int32, k_dev)
    same = plane[:, :, None] == plane[:, None, :]
    earlier = order[None, None, :] < order[None, :, None]
    rank = jnp.sum((same & earlier).astype(jnp.int32), axis=2)
    return plane, rank


def send_parts(plane, first_plane, meta, box, n_dev):
    blk_plane, blk_row, blk_col, frac_plane, frac_row, defocus = meta
    n_blk = blk_plane.shape[1]
    own, n_rows, x = plane.shape
    plane_of, rank = slot_tables(blk_plane, n_dev)
    k_dev = plane_of.shape[1]
    t = lax.iota(jnp.int32, own)[:, None, None, None]
    side = lax.iota(jnp.int32, 2)[None, None, :, None]
    u = lax.iota(jnp.int32, 2)[None, None, None, :]
    target = first_plane + t - side
    match = (plane_of[None, :, None, None, :] == target[..., None]) & (
        rank[None, :, None, None, :] == u[..., None]
    )
    valid = jnp.any(match, axis=-1)
    def pick(values):
        table = values.reshape(n_dev, k_dev)[None, :, None, None, :]
        return jnp.sum(jnp.where(match, table, jnp.zeros_like(table)), axis=-1).reshape(-1)

    rows = pick(blk_row)
    cols = pick(blk_col)
    frac_z = pick(frac_plane)
    frac_y = pick(frac_row)[:, None]
    focus = pick(jnp.broadcast_to(defocus[:, None], blk_plane.shape))
    side_f = jnp.broadcast_to(side, (own, n_dev, 2, 2)).reshape(-1)
    valid = valid.reshape(-1)
    lane = lax.iota(jnp.int32, LANES)
    column_x = cols[:, None] * LANES + lane[None, :]
    fold_x = jnp.minimum(column_x, box - column_x).astype(jnp.float32)
    fold_y = jnp.minimum(rows, box - rows).astype(jnp.float32)
    wave_sq = (fold_x * fold_x + (fold_y * fold_y)[:, None]) / float(box * box)
    ctf_value = -jnp.sin(CTF_SCALE * focus[:, None] * wave_sq + CTF_PHASE)
    weight = jnp.where(side_f == 0, 1.0 - frac_z, frac_z)
    weight = jnp.where(valid, weight, 0.0)
    scale = weight[:, None] * ctf_value
    step = int(math.isqrt(n_rows))
    a = lax.iota(jnp.int32, n_rows // step)[None, :]
    b = lax.iota(jnp.int32, step)[None, :]

    def row_roots(r):
        a_re, a_im = roots(r[:, None], a * step, n_rows, 1.0)
        b_re, b_im = roots(r[:, None], b, n_rows, 1.0)
        w_re = a_re[:, :, None] * b_re[:, None, :] - a_im[:, :, None] * b_im[:, None, :]
        w_im = a_re[:, :, None] * b_im[:, None, :] + a_im[:, :, None] * b_re[:, None, :]
        return w_re.reshape(-1, n_rows), w_im.reshape(-1, n_rows)

    lo_re, lo_im = row_roots(rows)
    hi_re, hi_im = row_roots(rows + 1)
    norm = 1.0 / math.sqrt(n_rows)
    w_re = ((1.0 - frac_y) * lo_re + frac_y * hi_re) * norm
    w_im = ((1.0 - frac_y) * lo_im + frac_y * hi_im) * norm
    n_s = w_re.shape[0] // own
    w_all = jnp.stack([w_re.reshape(own, n_s, n_rows), w_im.reshape(own, n_s, n_rows)], axis=1)
    r_t = jnp.einsum("trc,tpsr->tpcs", plane, w_all, precision=MID)
    m = x // SPLIT
    r5 = r_t.reshape(own, 2, m, SPLIT, n_s)
    idx = lax.iota(jnp.int32, m)
    c_re, c_im = roots(idx[:, None], idx[None, :], m, 1.0 / math.sqrt(x))
    w_col = jnp.stack(
        [jnp.stack([c_re, -c_im], axis=1), jnp.stack([c_im, c_re], axis=1)], axis=0
    )
    y = jnp.einsum("qkpn,tpnjs->tqkjs", w_col, r5, precision=MID)
    y_re = y[:, 0]
    y_im = y[:, 1]
    n1 = lax.iota(jnp.int32, SPLIT)
    cols_t = cols.reshape(own, n_s)
    e_re, e_im = roots(n1[None, :, None], cols_t[:, None, :], SPLIT, 1.0)
    t_re, t_im = roots(lane[:, None], n1[None, :], box, 1.0)
    e_re = e_re[:, None]
    e_im = e_im[:, None]
    t_re = t_re[None, :, :, None]
    t_im = t_im[None, :, :, None]
    g_re = e_re * t_re - e_im * t_im
    g_im = e_re * t_im + e_im * t_re
    o_re = jnp.sum(g_re * y_re - g_im * y_im, axis=2)
    o_im = jnp.sum(g_re * y_im + g_im * y_re, axis=2)
    o_re = jnp.swapaxes(o_re, 1, 2).reshape(own * n_s, LANES)
    o_im = jnp.swapaxes(o_im, 1, 2).reshape(own * n_s, LANES)
    parts = jnp.stack([scale * o_re, scale * o_im], axis=1)
    parts = parts.reshape(own, n_dev, 4, 2, LANES)
    return jnp.swapaxes(parts, 0, 1).reshape(n_dev, own * 4, 2, LANES)


def gather_parts(recv, blk_plane, me, own, n_slab, n_img):
    n_dev = n_slab * n_img
    plane, rank = slot_tables(blk_plane, n_dev)
    mine = plane[me]
    my_rank = rank[me]
    slots = own * 4

    def place(q, side):
        holder = q // own
        src = (holder % n_slab) * n_img + holder // n_slab
        return src * slots + (q % own) * 4 + side * 2 + my_rank

    flat = recv.reshape(-1, 2, LANES)
    return flat[place(mine, 0)] + flat[place(mine + 1, 1)]


def on_device(volume, blk_plane, blk_row, blk_col, frac_plane, frac_row, defocus):
    box = volume.shape[2]
    n_slab = lax.axis_size("slab")
    n_img = lax.axis_size("img")
    n_dev = n_slab * n_img
    plane = lax.all_to_all(volume, "slab", split_axis=0, concat_axis=1, tiled=True)
    own = plane.shape[0]
    first_plane = (lax.axis_index("img") * n_slab + lax.axis_index("slab")) * own
    meta = (blk_plane, blk_row, blk_col, frac_plane, frac_row, defocus)
    parts = send_parts(plane, first_plane, meta, box, n_dev)
    parts = parts.reshape(n_slab, n_img, *parts.shape[1:])
    parts = lax.all_to_all(parts, "img", split_axis=1, concat_axis=1, tiled=True)
    recv = lax.all_to_all(parts, "slab", split_axis=0, concat_axis=0, tiled=True)
    me = lax.axis_index("slab") * n_img + lax.axis_index("img")
    total = gather_parts(recv, blk_plane, me, own, n_slab, n_img)
    n_blk = blk_plane.shape[1]
    return total.reshape(-1, n_blk, 2, LANES)


def solution(mesh):
    placed = (P("img", "slab", None), P(), P(), P(), P(), P(), P())
    return jax.shard_map(
        on_device,
        mesh=mesh,
        in_specs=placed,
        out_specs=P(("slab", "img"), None, None, None),
        check_vma=False,
    )
```

```python
import math

import jax
import jax.numpy as jnp
from jax import lax
from jax.sharding import PartitionSpec as P

LANES = 128
SPLIT = 8
CHUNKS = 2


CTF_SCALE = 20.0
CTF_PHASE = 0.07
MID = lax.Precision.HIGH


def roots(rows, cols, length, factor):
    phase = rows * cols % length
    angle = phase.astype(jnp.float32) * (2.0 * math.pi / length)
    return (jnp.cos(angle) * factor, -jnp.sin(angle) * factor)


def slot_tables(blk_plane, n_dev):
    plane = blk_plane.reshape(n_dev, -1)
    k_dev = plane.shape[1]
    order = lax.iota(jnp.int32, k_dev)
    same = plane[:, :, None] == plane[:, None, :]
    earlier = order[None, None, :] < order[None, :, None]
    rank = jnp.sum((same & earlier).astype(jnp.int32), axis=2)
    return plane, rank


def send_parts(planes, first_plane, meta, box, n_dev):
    blk_plane, blk_row, blk_col, frac_plane, frac_row, defocus = meta
    n_blk = blk_plane.shape[1]
    own, n_rows, width = planes[0].shape
    x = width * len(planes)
    plane_of, rank = slot_tables(blk_plane, n_dev)
    k_dev = plane_of.shape[1]
    t = lax.iota(jnp.int32, own)[:, None, None, None]
    side = lax.iota(jnp.int32, 2)[None, None, :, None]
    u = lax.iota(jnp.int32, 2)[None, None, None, :]
    target = first_plane + t - side
    match = (plane_of[None, :, None, None, :] == target[..., None]) & (
        rank[None, :, None, None, :] == u[..., None]
    )
    valid = jnp.any(match, axis=-1)
    def pick(values):
        table = values.reshape(n_dev, k_dev)[None, :, None, None, :]
        return jnp.sum(jnp.where(match, table, jnp.zeros_like(table)), axis=-1).reshape(-1)

    rows = pick(blk_row)
    cols = pick(blk_col)
    frac_z = pick(frac_plane)
    frac_y = pick(frac_row)[:, None]
    focus = pick(jnp.broadcast_to(defocus[:, None], blk_plane.shape))
    side_f = jnp.broadcast_to(side, (own, n_dev, 2, 2)).reshape(-1)
    valid = valid.reshape(-1)
    lane = lax.iota(jnp.int32, LANES)
    column_x = cols[:, None] * LANES + lane[None, :]
    fold_x = jnp.minimum(column_x, box - column_x).astype(jnp.float32)
    fold_y = jnp.minimum(rows, box - rows).astype(jnp.float32)
    wave_sq = (fold_x * fold_x + (fold_y * fold_y)[:, None]) / float(box * box)
    ctf_value = -jnp.sin(CTF_SCALE * focus[:, None] * wave_sq + CTF_PHASE)
    weight = jnp.where(side_f == 0, 1.0 - frac_z, frac_z)
    weight = jnp.where(valid, weight, 0.0)
    scale = weight[:, None] * ctf_value
    step = int(math.isqrt(n_rows))
    a = lax.iota(jnp.int32, n_rows // step)[None, :]
    b = lax.iota(jnp.int32, step)[None, :]

    def row_roots(r):
        a_re, a_im = roots(r[:, None], a * step, n_rows, 1.0)
        b_re, b_im = roots(r[:, None], b, n_rows, 1.0)
        w_re = a_re[:, :, None] * b_re[:, None, :] - a_im[:, :, None] * b_im[:, None, :]
        w_im = a_re[:, :, None] * b_im[:, None, :] + a_im[:, :, None] * b_re[:, None, :]
        return w_re.reshape(-1, n_rows), w_im.reshape(-1, n_rows)

    lo_re, lo_im = row_roots(rows)
    hi_re, hi_im = row_roots(rows + 1)
    norm = 1.0 / math.sqrt(n_rows)
    w_re = ((1.0 - frac_y) * lo_re + frac_y * hi_re) * norm
    w_im = ((1.0 - frac_y) * lo_im + frac_y * hi_im) * norm
    n_s = w_re.shape[0] // own
    w_all = jnp.stack([w_re.reshape(own, n_s, n_rows), w_im.reshape(own, n_s, n_rows)], axis=1)
    m = x // SPLIT
    step_n2 = m // len(planes)
    idx = lax.iota(jnp.int32, m)
    c_re, c_im = roots(idx[:, None], idx[None, :], m, 1.0 / math.sqrt(x))
    w_col = jnp.stack(
        [jnp.stack([c_re, -c_im], axis=1), jnp.stack([c_im, c_re], axis=1)], axis=0
    )
    y = None
    for j, piece in enumerate(planes):
        r_t = jnp.einsum("trc,tpsr->tpcs", piece, w_all, precision=MID)
        r5 = r_t.reshape(own, 2, step_n2, SPLIT, n_s)
        w_j = w_col[:, :, :, j * step_n2:(j + 1) * step_n2]
        y_j = jnp.einsum("qkpn,tpnjs->tqkjs", w_j, r5, precision=MID)
        y = y_j if y is None else y + y_j
    y_re = y[:, 0]
    y_im = y[:, 1]
    n1 = lax.iota(jnp.int32, SPLIT)
    cols_t = cols.reshape(own, n_s)
    e_re, e_im = roots(n1[None, :, None], cols_t[:, None, :], SPLIT, 1.0)
    t_re, t_im = roots(lane[:, None], n1[None, :], box, 1.0)
    e_re = e_re[:, None]
    e_im = e_im[:, None]
    t_re = t_re[None, :, :, None]
    t_im = t_im[None, :, :, None]
    g_re = e_re * t_re - e_im * t_im
    g_im = e_re * t_im + e_im * t_re
    o_re = jnp.sum(g_re * y_re - g_im * y_im, axis=2)
    o_im = jnp.sum(g_re * y_im + g_im * y_re, axis=2)
    o_re = jnp.swapaxes(o_re, 1, 2).reshape(own * n_s, LANES)
    o_im = jnp.swapaxes(o_im, 1, 2).reshape(own * n_s, LANES)
    parts = jnp.stack([scale * o_re, scale * o_im], axis=1)
    parts = parts.reshape(own, n_dev, 4, 2, LANES)
    return jnp.swapaxes(parts, 0, 1).reshape(n_dev, own * 4, 2, LANES)


def gather_parts(recv, blk_plane, me, own, n_slab, n_img):
    n_dev = n_slab * n_img
    plane, rank = slot_tables(blk_plane, n_dev)
    mine = plane[me]
    my_rank = rank[me]
    slots = own * 4

    def place(q, side):
        holder = q // own
        src = (holder % n_slab) * n_img + holder // n_slab
        return src * slots + (q % own) * 4 + side * 2 + my_rank

    flat = recv.reshape(-1, 2, LANES)
    return flat[place(mine, 0)] + flat[place(mine + 1, 1)]


def on_device(volume, blk_plane, blk_row, blk_col, frac_plane, frac_row, defocus):
    box = volume.shape[2]
    n_slab = lax.axis_size("slab")
    n_img = lax.axis_size("img")
    n_dev = n_slab * n_img
    width = box // CHUNKS
    planes = [
        lax.all_to_all(
            volume[:, :, j * width:(j + 1) * width], "slab", split_axis=0, concat_axis=1, tiled=True
        )
        for j in range(CHUNKS)
    ]
    own = planes[0].shape[0]
    first_plane = (lax.axis_index("img") * n_slab + lax.axis_index("slab")) * own
    meta = (blk_plane, blk_row, blk_col, frac_plane, frac_row, defocus)
    parts = send_parts(planes, first_plane, meta, box, n_dev)
    recv = lax.all_to_all(parts, ("slab", "img"), split_axis=0, concat_axis=0, tiled=True)
    me = lax.axis_index("slab") * n_img + lax.axis_index("img")
    total = gather_parts(recv, blk_plane, me, own, n_slab, n_img)
    n_blk = blk_plane.shape[1]
    return total.reshape(-1, n_blk, 2, LANES)


def solution(mesh):
    placed = (P("img", "slab", None), P(), P(), P(), P(), P(), P())
    return jax.shard_map(
        on_device,
        mesh=mesh,
        in_specs=placed,
        out_specs=P(("slab", "img"), None, None, None),
        check_vma=False,
    )
```

```python
import math

import jax
import jax.numpy as jnp
from jax import lax
from jax.sharding import PartitionSpec as P

LANES = 128
SPLIT = 8


CTF_SCALE = 20.0
CTF_PHASE = 0.07
MID = lax.Precision.HIGH


def roots(rows, cols, length, factor):
    phase = rows * cols % length
    angle = phase.astype(jnp.float32) * (2.0 * math.pi / length)
    return (jnp.cos(angle) * factor, -jnp.sin(angle) * factor)


def slot_tables(blk_plane, n_dev):
    plane = blk_plane.reshape(n_dev, -1)
    k_dev = plane.shape[1]
    order = lax.iota(jnp.int32, k_dev)
    same = plane[:, :, None] == plane[:, None, :]
    earlier = order[None, None, :] < order[None, :, None]
    rank = jnp.sum((same & earlier).astype(jnp.int32), axis=2)
    return plane, rank


def send_parts(planes, first_plane, meta, box, n_dev):
    blk_plane, blk_row, blk_col, frac_plane, frac_row, defocus = meta
    n_blk = blk_plane.shape[1]
    own, n_rows, width = planes[0].shape
    x = width * len(planes)
    plane_of, rank = slot_tables(blk_plane, n_dev)
    k_dev = plane_of.shape[1]
    t = lax.iota(jnp.int32, own)[:, None, None, None]
    side = lax.iota(jnp.int32, 2)[None, None, :, None]
    u = lax.iota(jnp.int32, 2)[None, None, None, :]
    target = first_plane + t - side
    match = (plane_of[None, :, None, None, :] == target[..., None]) & (
        rank[None, :, None, None, :] == u[..., None]
    )
    valid = jnp.any(match, axis=-1)
    def pick(values):
        table = values.reshape(n_dev, k_dev)[None, :, None, None, :]
        return jnp.sum(jnp.where(match, table, jnp.zeros_like(table)), axis=-1).reshape(-1)

    rows = pick(blk_row)
    cols = pick(blk_col)
    frac_z = pick(frac_plane)
    frac_y = pick(frac_row)[:, None]
    focus = pick(jnp.broadcast_to(defocus[:, None], blk_plane.shape))
    side_f = jnp.broadcast_to(side, (own, n_dev, 2, 2)).reshape(-1)
    valid = valid.reshape(-1)
    lane = lax.iota(jnp.int32, LANES)
    column_x = cols[:, None] * LANES + lane[None, :]
    fold_x = jnp.minimum(column_x, box - column_x).astype(jnp.float32)
    fold_y = jnp.minimum(rows, box - rows).astype(jnp.float32)
    wave_sq = (fold_x * fold_x + (fold_y * fold_y)[:, None]) / float(box * box)
    ctf_value = -jnp.sin(CTF_SCALE * focus[:, None] * wave_sq + CTF_PHASE)
    weight = jnp.where(side_f == 0, 1.0 - frac_z, frac_z)
    weight = jnp.where(valid, weight, 0.0)
    scale = weight[:, None] * ctf_value
    step = int(math.isqrt(n_rows))
    a = lax.iota(jnp.int32, n_rows // step)[None, :]
    b = lax.iota(jnp.int32, step)[None, :]

    def row_roots(r):
        a_re, a_im = roots(r[:, None], a * step, n_rows, 1.0)
        b_re, b_im = roots(r[:, None], b, n_rows, 1.0)
        w_re = a_re[:, :, None] * b_re[:, None, :] - a_im[:, :, None] * b_im[:, None, :]
        w_im = a_re[:, :, None] * b_im[:, None, :] + a_im[:, :, None] * b_re[:, None, :]
        return w_re.reshape(-1, n_rows), w_im.reshape(-1, n_rows)

    lo_re, lo_im = row_roots(rows)
    hi_re, hi_im = row_roots(rows + 1)
    norm = 1.0 / math.sqrt(n_rows)
    w_re = ((1.0 - frac_y) * lo_re + frac_y * hi_re) * norm
    w_im = ((1.0 - frac_y) * lo_im + frac_y * hi_im) * norm
    n_s = w_re.shape[0] // own
    w_all = jnp.stack([w_re.reshape(own, n_s, n_rows), w_im.reshape(own, n_s, n_rows)], axis=1)
    m = x // SPLIT
    step_n2 = m // len(planes)
    idx = lax.iota(jnp.int32, m)
    c_re, c_im = roots(idx[:, None], idx[None, :], m, 1.0 / math.sqrt(x))
    w_col = jnp.stack(
        [jnp.stack([c_re, -c_im], axis=1), jnp.stack([c_im, c_re], axis=1)], axis=0
    )
    y = None
    for j, piece in enumerate(planes):
        r_t = jnp.einsum("trc,tpsr->tpcs", piece, w_all, precision=MID)
        r5 = r_t.reshape(own, 2, step_n2, SPLIT, n_s)
        w_j = w_col[:, :, :, j * step_n2:(j + 1) * step_n2]
        y_j = jnp.einsum("qkpn,tpnjs->tqkjs", w_j, r5, precision=MID)
        y = y_j if y is None else y + y_j
    y_re = y[:, 0]
    y_im = y[:, 1]
    n1 = lax.iota(jnp.int32, SPLIT)
    cols_t = cols.reshape(own, n_s)
    e_re, e_im = roots(n1[None, :, None], cols_t[:, None, :], SPLIT, 1.0)
    t_re, t_im = roots(lane[:, None], n1[None, :], box, 1.0)
    e_re = e_re[:, None]
    e_im = e_im[:, None]
    t_re = t_re[None, :, :, None]
    t_im = t_im[None, :, :, None]
    g_re = e_re * t_re - e_im * t_im
    g_im = e_re * t_im + e_im * t_re
    o_re = jnp.sum(g_re * y_re - g_im * y_im, axis=2)
    o_im = jnp.sum(g_re * y_im + g_im * y_re, axis=2)
    o_re = jnp.swapaxes(o_re, 1, 2).reshape(own * n_s, LANES)
    o_im = jnp.swapaxes(o_im, 1, 2).reshape(own * n_s, LANES)
    parts = jnp.stack([scale * o_re, scale * o_im], axis=1)
    parts = parts.reshape(own, n_dev, 4, 2, LANES)
    return jnp.swapaxes(parts, 0, 1).reshape(n_dev, own * 4, 2, LANES)


def gather_parts(recv, blk_plane, me, own, n_slab, n_img):
    n_dev = n_slab * n_img
    plane, rank = slot_tables(blk_plane, n_dev)
    mine = plane[me]
    my_rank = rank[me]
    slots = own * 4

    def place(q, side):
        holder = q // own
        src = (holder % n_slab) * n_img + holder // n_slab
        return src * slots + (q % own) * 4 + side * 2 + my_rank

    flat = recv.reshape(-1, 2, LANES)
    return flat[place(mine, 0)] + flat[place(mine + 1, 1)]


def on_device(volume, blk_plane, blk_row, blk_col, frac_plane, frac_row, defocus):
    box = volume.shape[2]
    n_slab = lax.axis_size("slab")
    n_img = lax.axis_size("img")
    n_dev = n_slab * n_img
    planes = [lax.all_to_all(volume, "slab", split_axis=0, concat_axis=1, tiled=True)]
    own = planes[0].shape[0]
    first_plane = (lax.axis_index("img") * n_slab + lax.axis_index("slab")) * own
    meta = (blk_plane, blk_row, blk_col, frac_plane, frac_row, defocus)
    parts = send_parts(planes, first_plane, meta, box, n_dev)
    recv = lax.all_to_all(parts, ("slab", "img"), split_axis=0, concat_axis=0, tiled=True)
    me = lax.axis_index("slab") * n_img + lax.axis_index("img")
    total = gather_parts(recv, blk_plane, me, own, n_slab, n_img)
    n_blk = blk_plane.shape[1]
    return total.reshape(-1, n_blk, 2, LANES)


def solution(mesh):
    placed = (P("img", "slab", None), P(), P(), P(), P(), P(), P())
    return jax.shard_map(
        on_device,
        mesh=mesh,
        in_specs=placed,
        out_specs=P(("slab", "img"), None, None, None),
        check_vma=False,
    )
```

```python
import math

import jax
import jax.numpy as jnp
from jax import lax
from jax.sharding import PartitionSpec as P

LANES = 128
SPLIT = 8


CTF_SCALE = 20.0
CTF_PHASE = 0.07
MID = lax.Precision.HIGH


def roots(rows, cols, length, factor):
    phase = rows * cols % length
    angle = phase.astype(jnp.float32) * (2.0 * math.pi / length)
    return (jnp.cos(angle) * factor, -jnp.sin(angle) * factor)


def slot_tables(blk_plane, n_dev):
    plane = blk_plane.reshape(n_dev, -1)
    k_dev = plane.shape[1]
    order = lax.iota(jnp.int32, k_dev)
    same = plane[:, :, None] == plane[:, None, :]
    earlier = order[None, None, :] < order[None, :, None]
    rank = jnp.sum((same & earlier).astype(jnp.int32), axis=2)
    return plane, rank


def send_parts(planes, first_plane, meta, box, n_dev):
    blk_plane, blk_row, blk_col, frac_plane, frac_row, defocus = meta
    n_blk = blk_plane.shape[1]
    own, n_rows, width = planes[0].shape
    x = width * len(planes)
    plane_of, rank = slot_tables(blk_plane, n_dev)
    k_dev = plane_of.shape[1]
    t = lax.iota(jnp.int32, own)[:, None, None, None]
    side = lax.iota(jnp.int32, 2)[None, None, :, None]
    u = lax.iota(jnp.int32, 2)[None, None, None, :]
    target = first_plane + t - side
    match = (plane_of[None, :, None, None, :] == target[..., None]) & (
        rank[None, :, None, None, :] == u[..., None]
    )
    valid = jnp.any(match, axis=-1)
    def pick(values):
        table = values.reshape(n_dev, k_dev)[None, :, None, None, :]
        return jnp.sum(jnp.where(match, table, jnp.zeros_like(table)), axis=-1).reshape(-1)

    rows = pick(blk_row)
    cols = pick(blk_col)
    frac_z = pick(frac_plane)
    frac_y = pick(frac_row)[:, None]
    focus = pick(jnp.broadcast_to(defocus[:, None], blk_plane.shape))
    side_f = jnp.broadcast_to(side, (own, n_dev, 2, 2)).reshape(-1)
    valid = valid.reshape(-1)
    lane = lax.iota(jnp.int32, LANES)
    column_x = cols[:, None] * LANES + lane[None, :]
    fold_x = jnp.minimum(column_x, box - column_x).astype(jnp.float32)
    fold_y = jnp.minimum(rows, box - rows).astype(jnp.float32)
    wave_sq = (fold_x * fold_x + (fold_y * fold_y)[:, None]) / float(box * box)
    ctf_value = -jnp.sin(CTF_SCALE * focus[:, None] * wave_sq + CTF_PHASE)
    weight = jnp.where(side_f == 0, 1.0 - frac_z, frac_z)
    weight = jnp.where(valid, weight, 0.0)
    scale = weight[:, None] * ctf_value
    step = int(math.isqrt(n_rows))
    a = lax.iota(jnp.int32, n_rows // step)[None, :]
    b = lax.iota(jnp.int32, step)[None, :]

    def row_roots(r):
        a_re, a_im = roots(r[:, None], a * step, n_rows, 1.0)
        b_re, b_im = roots(r[:, None], b, n_rows, 1.0)
        w_re = a_re[:, :, None] * b_re[:, None, :] - a_im[:, :, None] * b_im[:, None, :]
        w_im = a_re[:, :, None] * b_im[:, None, :] + a_im[:, :, None] * b_re[:, None, :]
        return w_re.reshape(-1, n_rows), w_im.reshape(-1, n_rows)

    lo_re, lo_im = row_roots(rows)
    hi_re, hi_im = row_roots(rows + 1)
    norm = 1.0 / math.sqrt(n_rows)
    w_re = ((1.0 - frac_y) * lo_re + frac_y * hi_re) * norm
    w_im = ((1.0 - frac_y) * lo_im + frac_y * hi_im) * norm
    n_s = w_re.shape[0] // own
    w_all = jnp.stack([w_re.reshape(own, n_s, n_rows), w_im.reshape(own, n_s, n_rows)], axis=1)
    m = x // SPLIT
    step_n2 = m // len(planes)
    idx = lax.iota(jnp.int32, m)
    c_re, c_im = roots(idx[:, None], idx[None, :], m, 1.0 / math.sqrt(x))
    w_col = jnp.stack(
        [jnp.stack([c_re, -c_im], axis=1), jnp.stack([c_im, c_re], axis=1)], axis=0
    )
    y = None
    for j, piece in enumerate(planes):
        r_t = jnp.einsum("trc,tpsr->tpcs", piece, w_all, precision=MID)
        r5 = r_t.reshape(own, 2, step_n2, SPLIT, n_s)
        w_j = w_col[:, :, :, j * step_n2:(j + 1) * step_n2]
        y_j = jnp.einsum("qkpn,tpnjs->tqkjs", w_j, r5, precision=MID)
        y = y_j if y is None else y + y_j
    y_re = y[:, 0]
    y_im = y[:, 1]
    n1 = lax.iota(jnp.int32, SPLIT)
    cols_t = cols.reshape(own, n_s)
    e_re, e_im = roots(n1[None, :, None], cols_t[:, None, :], SPLIT, 1.0)
    t_re, t_im = roots(lane[:, None], n1[None, :], box, 1.0)
    e_re = e_re[:, None]
    e_im = e_im[:, None]
    t_re = t_re[None, :, :, None]
    t_im = t_im[None, :, :, None]
    g_re = e_re * t_re - e_im * t_im
    g_im = e_re * t_im + e_im * t_re
    o_re = jnp.sum(g_re * y_re - g_im * y_im, axis=2)
    o_im = jnp.sum(g_re * y_im + g_im * y_re, axis=2)
    o_re = jnp.swapaxes(o_re, 1, 2).reshape(own * n_s, LANES)
    o_im = jnp.swapaxes(o_im, 1, 2).reshape(own * n_s, LANES)
    parts = jnp.concatenate([scale * o_re, scale * o_im], axis=1)
    parts = parts.reshape(own, n_dev, 4 * 2 * LANES)
    return jnp.swapaxes(parts, 0, 1).reshape(n_dev, own * 4 * 2 * LANES)


def gather_parts(recv, blk_plane, me, own, n_slab, n_img):
    n_dev = n_slab * n_img
    plane, rank = slot_tables(blk_plane, n_dev)
    mine = plane[me]
    my_rank = rank[me]
    slots = own * 4

    def place(q, side):
        holder = q // own
        src = (holder % n_slab) * n_img + holder // n_slab
        return src * slots + (q % own) * 4 + side * 2 + my_rank

    flat = recv.reshape(-1, 2, LANES)
    return flat[place(mine, 0)] + flat[place(mine + 1, 1)]


def on_device(volume, blk_plane, blk_row, blk_col, frac_plane, frac_row, defocus):
    box = volume.shape[2]
    n_slab = lax.axis_size("slab")
    n_img = lax.axis_size("img")
    n_dev = n_slab * n_img
    planes = [lax.all_to_all(volume, "slab", split_axis=0, concat_axis=1, tiled=True)]
    own = planes[0].shape[0]
    first_plane = (lax.axis_index("img") * n_slab + lax.axis_index("slab")) * own
    meta = (blk_plane, blk_row, blk_col, frac_plane, frac_row, defocus)
    parts = send_parts(planes, first_plane, meta, box, n_dev)
    recv = lax.all_to_all(parts, ("slab", "img"), split_axis=0, concat_axis=0, tiled=True)
    me = lax.axis_index("slab") * n_img + lax.axis_index("img")
    total = gather_parts(recv, blk_plane, me, own, n_slab, n_img)
    n_blk = blk_plane.shape[1]
    return total.reshape(-1, n_blk, 2, LANES)


def solution(mesh):
    placed = (P("img", "slab", None), P(), P(), P(), P(), P(), P())
    return jax.shard_map(
        on_device,
        mesh=mesh,
        in_specs=placed,
        out_specs=P(("slab", "img"), None, None, None),
        check_vma=False,
    )
```

```python
import math

import jax
import jax.numpy as jnp
from jax import lax
from jax.sharding import PartitionSpec as P
from jax.experimental.layout import Layout, with_layout_constraint

LANES = 128
SPLIT = 8


CTF_SCALE = 20.0
CTF_PHASE = 0.07
MID = lax.Precision.HIGH


def roots(rows, cols, length, factor):
    phase = rows * cols % length
    angle = phase.astype(jnp.float32) * (2.0 * math.pi / length)
    return (jnp.cos(angle) * factor, -jnp.sin(angle) * factor)


def slot_tables(blk_plane, n_dev):
    plane = blk_plane.reshape(n_dev, -1)
    k_dev = plane.shape[1]
    order = lax.iota(jnp.int32, k_dev)
    same = plane[:, :, None] == plane[:, None, :]
    earlier = order[None, None, :] < order[None, :, None]
    rank = jnp.sum((same & earlier).astype(jnp.int32), axis=2)
    return plane, rank


def send_parts(planes, first_plane, meta, box, n_dev):
    blk_plane, blk_row, blk_col, frac_plane, frac_row, defocus = meta
    n_blk = blk_plane.shape[1]
    own, n_rows, width = planes[0].shape
    x = width * len(planes)
    plane_of, rank = slot_tables(blk_plane, n_dev)
    k_dev = plane_of.shape[1]
    t = lax.iota(jnp.int32, own)[:, None, None, None]
    side = lax.iota(jnp.int32, 2)[None, None, :, None]
    u = lax.iota(jnp.int32, 2)[None, None, None, :]
    target = first_plane + t - side
    match = (plane_of[None, :, None, None, :] == target[..., None]) & (
        rank[None, :, None, None, :] == u[..., None]
    )
    valid = jnp.any(match, axis=-1)
    def pick(values):
        table = values.reshape(n_dev, k_dev)[None, :, None, None, :]
        return jnp.sum(jnp.where(match, table, jnp.zeros_like(table)), axis=-1).reshape(-1)

    rows = pick(blk_row)
    cols = pick(blk_col)
    frac_z = pick(frac_plane)
    frac_y = pick(frac_row)[:, None]
    focus = pick(jnp.broadcast_to(defocus[:, None], blk_plane.shape))
    side_f = jnp.broadcast_to(side, (own, n_dev, 2, 2)).reshape(-1)
    valid = valid.reshape(-1)
    lane = lax.iota(jnp.int32, LANES)
    column_x = cols[:, None] * LANES + lane[None, :]
    fold_x = jnp.minimum(column_x, box - column_x).astype(jnp.float32)
    fold_y = jnp.minimum(rows, box - rows).astype(jnp.float32)
    wave_sq = (fold_x * fold_x + (fold_y * fold_y)[:, None]) / float(box * box)
    ctf_value = -jnp.sin(CTF_SCALE * focus[:, None] * wave_sq + CTF_PHASE)
    weight = jnp.where(side_f == 0, 1.0 - frac_z, frac_z)
    weight = jnp.where(valid, weight, 0.0)
    scale = weight[:, None] * ctf_value
    step = int(math.isqrt(n_rows))
    a = lax.iota(jnp.int32, n_rows // step)[None, :]
    b = lax.iota(jnp.int32, step)[None, :]

    def row_roots(r):
        a_re, a_im = roots(r[:, None], a * step, n_rows, 1.0)
        b_re, b_im = roots(r[:, None], b, n_rows, 1.0)
        w_re = a_re[:, :, None] * b_re[:, None, :] - a_im[:, :, None] * b_im[:, None, :]
        w_im = a_re[:, :, None] * b_im[:, None, :] + a_im[:, :, None] * b_re[:, None, :]
        return w_re.reshape(-1, n_rows), w_im.reshape(-1, n_rows)

    lo_re, lo_im = row_roots(rows)
    hi_re, hi_im = row_roots(rows + 1)
    norm = 1.0 / math.sqrt(n_rows)
    w_re = ((1.0 - frac_y) * lo_re + frac_y * hi_re) * norm
    w_im = ((1.0 - frac_y) * lo_im + frac_y * hi_im) * norm
    n_s = w_re.shape[0] // own
    w_all = jnp.stack([w_re.reshape(own, n_s, n_rows), w_im.reshape(own, n_s, n_rows)], axis=1)
    m = x // SPLIT
    step_n2 = m // len(planes)
    idx = lax.iota(jnp.int32, m)
    c_re, c_im = roots(idx[:, None], idx[None, :], m, 1.0 / math.sqrt(x))
    w_col = jnp.stack(
        [jnp.stack([c_re, -c_im], axis=1), jnp.stack([c_im, c_re], axis=1)], axis=0
    )
    y = None
    for j, piece in enumerate(planes):
        r_t = jnp.einsum("trc,tpsr->tpcs", piece, w_all, precision=MID)
        r_t = with_layout_constraint(r_t, Layout(major_to_minor=(0, 1, 2, 3)))
        r5 = r_t.reshape(own, 2, step_n2, SPLIT, n_s)
        w_j = w_col[:, :, :, j * step_n2:(j + 1) * step_n2]
        y_j = jnp.einsum("qkpn,tpnjs->tqkjs", w_j, r5, precision=MID)
        y = y_j if y is None else y + y_j
    y_re = y[:, 0]
    y_im = y[:, 1]
    n1 = lax.iota(jnp.int32, SPLIT)
    cols_t = cols.reshape(own, n_s)
    e_re, e_im = roots(n1[None, :, None], cols_t[:, None, :], SPLIT, 1.0)
    t_re, t_im = roots(lane[:, None], n1[None, :], box, 1.0)
    e_re = e_re[:, None]
    e_im = e_im[:, None]
    t_re = t_re[None, :, :, None]
    t_im = t_im[None, :, :, None]
    g_re = e_re * t_re - e_im * t_im
    g_im = e_re * t_im + e_im * t_re
    o_re = jnp.sum(g_re * y_re - g_im * y_im, axis=2)
    o_im = jnp.sum(g_re * y_im + g_im * y_re, axis=2)
    o_re = jnp.swapaxes(o_re, 1, 2).reshape(own * n_s, LANES)
    o_im = jnp.swapaxes(o_im, 1, 2).reshape(own * n_s, LANES)
    parts = jnp.stack([scale * o_re, scale * o_im], axis=1)
    parts = parts.reshape(own, n_dev, 4, 2, LANES)
    return jnp.swapaxes(parts, 0, 1).reshape(n_dev, own * 4, 2, LANES)


def gather_parts(recv, blk_plane, me, own, n_slab, n_img):
    n_dev = n_slab * n_img
    plane, rank = slot_tables(blk_plane, n_dev)
    mine = plane[me]
    my_rank = rank[me]
    slots = own * 4

    def place(q, side):
        holder = q // own
        src = (holder % n_slab) * n_img + holder // n_slab
        return src * slots + (q % own) * 4 + side * 2 + my_rank

    flat = recv.reshape(-1, 2, LANES)
    return flat[place(mine, 0)] + flat[place(mine + 1, 1)]


def on_device(volume, blk_plane, blk_row, blk_col, frac_plane, frac_row, defocus):
    box = volume.shape[2]
    n_slab = lax.axis_size("slab")
    n_img = lax.axis_size("img")
    n_dev = n_slab * n_img
    planes = [lax.all_to_all(volume, "slab", split_axis=0, concat_axis=1, tiled=True)]
    own = planes[0].shape[0]
    first_plane = (lax.axis_index("img") * n_slab + lax.axis_index("slab")) * own
    meta = (blk_plane, blk_row, blk_col, frac_plane, frac_row, defocus)
    parts = send_parts(planes, first_plane, meta, box, n_dev)
    recv = lax.all_to_all(parts, ("slab", "img"), split_axis=0, concat_axis=0, tiled=True)
    me = lax.axis_index("slab") * n_img + lax.axis_index("img")
    total = gather_parts(recv, blk_plane, me, own, n_slab, n_img)
    n_blk = blk_plane.shape[1]
    return total.reshape(-1, n_blk, 2, LANES)


def solution(mesh):
    placed = (P("img", "slab", None), P(), P(), P(), P(), P(), P())
    return jax.shard_map(
        on_device,
        mesh=mesh,
        in_specs=placed,
        out_specs=P(("slab", "img"), None, None, None),
        check_vma=False,
    )
```

```python
import math

import jax
import jax.numpy as jnp
from jax import lax
from jax.sharding import PartitionSpec as P
from jax.experimental.layout import Layout, with_layout_constraint

LANES = 128
SPLIT = 8


CTF_SCALE = 20.0
CTF_PHASE = 0.07
MID = lax.Precision.HIGH


def roots(rows, cols, length, factor):
    phase = rows * cols % length
    angle = phase.astype(jnp.float32) * (2.0 * math.pi / length)
    return (jnp.cos(angle) * factor, -jnp.sin(angle) * factor)


def slot_tables(blk_plane, n_dev):
    plane = blk_plane.reshape(n_dev, -1)
    k_dev = plane.shape[1]
    order = lax.iota(jnp.int32, k_dev)
    same = plane[:, :, None] == plane[:, None, :]
    earlier = order[None, None, :] < order[None, :, None]
    rank = jnp.sum((same & earlier).astype(jnp.int32), axis=2)
    return plane, rank


def send_parts(planes, first_plane, meta, box, n_dev):
    blk_plane, blk_row, blk_col, frac_plane, frac_row, defocus = meta
    n_blk = blk_plane.shape[1]
    own, n_rows, width = planes[0].shape
    x = width * len(planes)
    plane_of, rank = slot_tables(blk_plane, n_dev)
    k_dev = plane_of.shape[1]
    t = lax.iota(jnp.int32, own)[:, None, None, None]
    side = lax.iota(jnp.int32, 2)[None, None, :, None]
    u = lax.iota(jnp.int32, 2)[None, None, None, :]
    target = first_plane + t - side
    match = (plane_of[None, :, None, None, :] == target[..., None]) & (
        rank[None, :, None, None, :] == u[..., None]
    )
    valid = jnp.any(match, axis=-1)
    def pick(values):
        table = values.reshape(n_dev, k_dev)[None, :, None, None, :]
        return jnp.sum(jnp.where(match, table, jnp.zeros_like(table)), axis=-1).reshape(-1)

    rows = pick(blk_row)
    cols = pick(blk_col)
    frac_z = pick(frac_plane)
    frac_y = pick(frac_row)[:, None]
    focus = pick(jnp.broadcast_to(defocus[:, None], blk_plane.shape))
    side_f = jnp.broadcast_to(side, (own, n_dev, 2, 2)).reshape(-1)
    valid = valid.reshape(-1)
    lane = lax.iota(jnp.int32, LANES)
    column_x = cols[:, None] * LANES + lane[None, :]
    fold_x = jnp.minimum(column_x, box - column_x).astype(jnp.float32)
    fold_y = jnp.minimum(rows, box - rows).astype(jnp.float32)
    wave_sq = (fold_x * fold_x + (fold_y * fold_y)[:, None]) / float(box * box)
    ctf_value = -jnp.sin(CTF_SCALE * focus[:, None] * wave_sq + CTF_PHASE)
    weight = jnp.where(side_f == 0, 1.0 - frac_z, frac_z)
    weight = jnp.where(valid, weight, 0.0)
    scale = weight[:, None] * ctf_value
    step = int(math.isqrt(n_rows))
    a = lax.iota(jnp.int32, n_rows // step)[None, :]
    b = lax.iota(jnp.int32, step)[None, :]

    def row_roots(r):
        a_re, a_im = roots(r[:, None], a * step, n_rows, 1.0)
        b_re, b_im = roots(r[:, None], b, n_rows, 1.0)
        w_re = a_re[:, :, None] * b_re[:, None, :] - a_im[:, :, None] * b_im[:, None, :]
        w_im = a_re[:, :, None] * b_im[:, None, :] + a_im[:, :, None] * b_re[:, None, :]
        return w_re.reshape(-1, n_rows), w_im.reshape(-1, n_rows)

    lo_re, lo_im = row_roots(rows)
    hi_re, hi_im = row_roots(rows + 1)
    norm = 1.0 / math.sqrt(n_rows)
    w_re = ((1.0 - frac_y) * lo_re + frac_y * hi_re) * norm
    w_im = ((1.0 - frac_y) * lo_im + frac_y * hi_im) * norm
    n_s = w_re.shape[0] // own
    w_all = jnp.stack([w_re.reshape(own, n_s, n_rows), w_im.reshape(own, n_s, n_rows)], axis=1)
    m = x // SPLIT
    step_n2 = m // len(planes)
    idx = lax.iota(jnp.int32, m)
    c_re, c_im = roots(idx[:, None], idx[None, :], m, 1.0 / math.sqrt(x))
    w_col = jnp.stack(
        [jnp.stack([c_re, -c_im], axis=1), jnp.stack([c_im, c_re], axis=1)], axis=0
    )
    y = None
    for j, piece in enumerate(planes):
        r_t = jnp.einsum("trc,tpsr->tpcs", piece, w_all, precision=MID)
        r_t = with_layout_constraint(r_t, Layout(major_to_minor=(0, 1, 2, 3)))
        r5 = r_t.reshape(own, 2, step_n2, SPLIT, n_s)
        w_j = w_col[:, :, :, j * step_n2:(j + 1) * step_n2]
        y_j = jnp.einsum("qkpn,tpnjs->tqkjs", w_j, r5, precision=MID)
        y = y_j if y is None else y + y_j
    y_re = y[:, 0]
    y_im = y[:, 1]
    n1 = lax.iota(jnp.int32, SPLIT)
    cols_t = cols.reshape(own, n_s)
    e_re, e_im = roots(n1[None, :, None], cols_t[:, None, :], SPLIT, 1.0)
    t_re, t_im = roots(lane[:, None], n1[None, :], box, 1.0)
    e_re = e_re[:, None]
    e_im = e_im[:, None]
    t_re = t_re[None, :, :, None]
    t_im = t_im[None, :, :, None]
    g_re = e_re * t_re - e_im * t_im
    g_im = e_re * t_im + e_im * t_re
    o_re = jnp.sum(g_re * y_re - g_im * y_im, axis=2)
    o_im = jnp.sum(g_re * y_im + g_im * y_re, axis=2)
    o_re = jnp.swapaxes(o_re, 1, 2).reshape(own * n_s, LANES)
    o_im = jnp.swapaxes(o_im, 1, 2).reshape(own * n_s, LANES)
    parts = jnp.stack([scale * o_re, scale * o_im], axis=1)
    parts = parts.reshape(own, n_dev, 4, 2, LANES)
    parts = jnp.swapaxes(parts, 0, 1).reshape(n_dev, own * 4, 2, LANES)
    return with_layout_constraint(parts, Layout(major_to_minor=(0, 1, 2, 3)))


def gather_parts(recv, blk_plane, me, own, n_slab, n_img):
    n_dev = n_slab * n_img
    plane, rank = slot_tables(blk_plane, n_dev)
    mine = plane[me]
    my_rank = rank[me]
    slots = own * 4

    def place(q, side):
        holder = q // own
        src = (holder % n_slab) * n_img + holder // n_slab
        return src * slots + (q % own) * 4 + side * 2 + my_rank

    flat = recv.reshape(-1, 2, LANES)
    return flat[place(mine, 0)] + flat[place(mine + 1, 1)]


def on_device(volume, blk_plane, blk_row, blk_col, frac_plane, frac_row, defocus):
    box = volume.shape[2]
    n_slab = lax.axis_size("slab")
    n_img = lax.axis_size("img")
    n_dev = n_slab * n_img
    planes = [lax.all_to_all(volume, "slab", split_axis=0, concat_axis=1, tiled=True)]
    own = planes[0].shape[0]
    first_plane = (lax.axis_index("img") * n_slab + lax.axis_index("slab")) * own
    meta = (blk_plane, blk_row, blk_col, frac_plane, frac_row, defocus)
    parts = send_parts(planes, first_plane, meta, box, n_dev)
    recv = lax.all_to_all(parts, ("slab", "img"), split_axis=0, concat_axis=0, tiled=True)
    me = lax.axis_index("slab") * n_img + lax.axis_index("img")
    total = gather_parts(recv, blk_plane, me, own, n_slab, n_img)
    n_blk = blk_plane.shape[1]
    return total.reshape(-1, n_blk, 2, LANES)


def solution(mesh):
    placed = (P("img", "slab", None), P(), P(), P(), P(), P(), P())
    return jax.shard_map(
        on_device,
        mesh=mesh,
        in_specs=placed,
        out_specs=P(("slab", "img"), None, None, None),
        check_vma=False,
    )
```

```python
import math

import jax
import jax.numpy as jnp
from jax import lax
from jax.sharding import Mesh, PartitionSpec as P
from jax.experimental.layout import Layout, with_layout_constraint

LANES = 128
SPLIT = 8


CTF_SCALE = 20.0
CTF_PHASE = 0.07
MID = lax.Precision.HIGH


def roots(rows, cols, length, factor):
    phase = rows * cols % length
    angle = phase.astype(jnp.float32) * (2.0 * math.pi / length)
    return (jnp.cos(angle) * factor, -jnp.sin(angle) * factor)


def slot_tables(blk_plane, n_dev):
    plane = blk_plane.reshape(n_dev, -1)
    k_dev = plane.shape[1]
    order = lax.iota(jnp.int32, k_dev)
    same = plane[:, :, None] == plane[:, None, :]
    earlier = order[None, None, :] < order[None, :, None]
    rank = jnp.sum((same & earlier).astype(jnp.int32), axis=2)
    return plane, rank


def send_parts(planes, first_plane, meta, box, n_dev):
    blk_plane, blk_row, blk_col, frac_plane, frac_row, defocus = meta
    n_blk = blk_plane.shape[1]
    own, n_rows, width = planes[0].shape
    x = width * len(planes)
    plane_of, rank = slot_tables(blk_plane, n_dev)
    k_dev = plane_of.shape[1]
    t = lax.iota(jnp.int32, own)[:, None, None, None]
    side = lax.iota(jnp.int32, 2)[None, None, :, None]
    u = lax.iota(jnp.int32, 2)[None, None, None, :]
    target = first_plane + t - side
    match = (plane_of[None, :, None, None, :] == target[..., None]) & (
        rank[None, :, None, None, :] == u[..., None]
    )
    valid = jnp.any(match, axis=-1)
    def pick(values):
        table = values.reshape(n_dev, k_dev)[None, :, None, None, :]
        return jnp.sum(jnp.where(match, table, jnp.zeros_like(table)), axis=-1).reshape(-1)

    rows = pick(blk_row)
    cols = pick(blk_col)
    frac_z = pick(frac_plane)
    frac_y = pick(frac_row)[:, None]
    focus = pick(jnp.broadcast_to(defocus[:, None], blk_plane.shape))
    side_f = jnp.broadcast_to(side, (own, n_dev, 2, 2)).reshape(-1)
    valid = valid.reshape(-1)
    lane = lax.iota(jnp.int32, LANES)
    column_x = cols[:, None] * LANES + lane[None, :]
    fold_x = jnp.minimum(column_x, box - column_x).astype(jnp.float32)
    fold_y = jnp.minimum(rows, box - rows).astype(jnp.float32)
    wave_sq = (fold_x * fold_x + (fold_y * fold_y)[:, None]) / float(box * box)
    ctf_value = -jnp.sin(CTF_SCALE * focus[:, None] * wave_sq + CTF_PHASE)
    weight = jnp.where(side_f == 0, 1.0 - frac_z, frac_z)
    weight = jnp.where(valid, weight, 0.0)
    scale = weight[:, None] * ctf_value
    step = int(math.isqrt(n_rows))
    a = lax.iota(jnp.int32, n_rows // step)[None, :]
    b = lax.iota(jnp.int32, step)[None, :]

    def row_roots(r):
        a_re, a_im = roots(r[:, None], a * step, n_rows, 1.0)
        b_re, b_im = roots(r[:, None], b, n_rows, 1.0)
        w_re = a_re[:, :, None] * b_re[:, None, :] - a_im[:, :, None] * b_im[:, None, :]
        w_im = a_re[:, :, None] * b_im[:, None, :] + a_im[:, :, None] * b_re[:, None, :]
        return w_re.reshape(-1, n_rows), w_im.reshape(-1, n_rows)

    lo_re, lo_im = row_roots(rows)
    hi_re, hi_im = row_roots(rows + 1)
    norm = 1.0 / math.sqrt(n_rows)
    w_re = ((1.0 - frac_y) * lo_re + frac_y * hi_re) * norm
    w_im = ((1.0 - frac_y) * lo_im + frac_y * hi_im) * norm
    n_s = w_re.shape[0] // own
    w_all = jnp.stack([w_re.reshape(own, n_s, n_rows), w_im.reshape(own, n_s, n_rows)], axis=1)
    m = x // SPLIT
    step_n2 = m // len(planes)
    idx = lax.iota(jnp.int32, m)
    c_re, c_im = roots(idx[:, None], idx[None, :], m, 1.0 / math.sqrt(x))
    w_col = jnp.stack(
        [jnp.stack([c_re, -c_im], axis=1), jnp.stack([c_im, c_re], axis=1)], axis=0
    )
    y = None
    for j, piece in enumerate(planes):
        r_t = jnp.einsum("trc,tpsr->tpcs", piece, w_all, precision=MID)
        r_t = with_layout_constraint(r_t, Layout(major_to_minor=(0, 1, 2, 3)))
        r5 = r_t.reshape(own, 2, step_n2, SPLIT, n_s)
        w_j = w_col[:, :, :, j * step_n2:(j + 1) * step_n2]
        y_j = jnp.einsum("qkpn,tpnjs->tqkjs", w_j, r5, precision=MID)
        y = y_j if y is None else y + y_j
    y_re = y[:, 0]
    y_im = y[:, 1]
    n1 = lax.iota(jnp.int32, SPLIT)
    cols_t = cols.reshape(own, n_s)
    e_re, e_im = roots(n1[None, :, None], cols_t[:, None, :], SPLIT, 1.0)
    t_re, t_im = roots(lane[:, None], n1[None, :], box, 1.0)
    e_re = e_re[:, None]
    e_im = e_im[:, None]
    t_re = t_re[None, :, :, None]
    t_im = t_im[None, :, :, None]
    g_re = e_re * t_re - e_im * t_im
    g_im = e_re * t_im + e_im * t_re
    o_re = jnp.sum(g_re * y_re - g_im * y_im, axis=2)
    o_im = jnp.sum(g_re * y_im + g_im * y_re, axis=2)
    o_re = jnp.swapaxes(o_re, 1, 2).reshape(own * n_s, LANES)
    o_im = jnp.swapaxes(o_im, 1, 2).reshape(own * n_s, LANES)
    parts = jnp.stack([scale * o_re, scale * o_im], axis=1)
    parts = parts.reshape(own, n_dev, 4, 2, LANES)
    return jnp.swapaxes(parts, 0, 1).reshape(n_dev, own * 4, 2, LANES)


def gather_parts(recv, blk_plane, me, own, n_slab, n_img):
    n_dev = n_slab * n_img
    plane, rank = slot_tables(blk_plane, n_dev)
    mine = plane[me]
    my_rank = rank[me]
    slots = own * 4

    def place(q, side):
        holder = q // own
        src = (holder % n_slab) * n_img + holder // n_slab
        return src * slots + (q % own) * 4 + side * 2 + my_rank

    flat = recv.reshape(-1, 2, LANES)
    return flat[place(mine, 0)] + flat[place(mine + 1, 1)]


def on_device(volume, blk_plane, blk_row, blk_col, frac_plane, frac_row, defocus):
    box = volume.shape[2]
    n_slab = lax.axis_size("chip") * lax.axis_size("core")
    n_img = lax.axis_size("img")
    n_dev = n_slab * n_img
    slab_index = lax.axis_index("chip") * lax.axis_size("core") + lax.axis_index("core")
    p_loc, r_loc, x = volume.shape
    n_chip = lax.axis_size("chip")
    own = p_loc // n_slab
    core = lax.axis_index("core")
    staged = volume.reshape(n_chip, 2, own, r_loc, x)
    staged = lax.all_to_all(staged, "chip", split_axis=0, concat_axis=0, tiled=True)
    mine = jnp.where(core == 0, staged[:, 0], staged[:, 1])
    other = jnp.where(core == 0, staged[:, 1], staged[:, 0])
    got = lax.ppermute(other, "core", perm=[(0, 1), (1, 0)])
    low = jnp.where(core == 0, mine, got)
    high = jnp.where(core == 0, got, mine)
    full = jnp.stack([low, high], axis=1)
    full = jnp.moveaxis(full, 2, 0)
    planes = [full.reshape(own, n_slab * r_loc, x)]
    first_plane = (lax.axis_index("img") * n_slab + slab_index) * own
    meta = (blk_plane, blk_row, blk_col, frac_plane, frac_row, defocus)
    parts = send_parts(planes, first_plane, meta, box, n_dev)
    recv = lax.all_to_all(parts, ("chip", "core", "img"), split_axis=0, concat_axis=0, tiled=True)
    me = slab_index * n_img + lax.axis_index("img")
    total = gather_parts(recv, blk_plane, me, own, n_slab, n_img)
    n_blk = blk_plane.shape[1]
    return total.reshape(-1, n_blk, 2, LANES)


def solution(mesh):
    slab, img = mesh.devices.shape
    split = Mesh(mesh.devices.reshape(slab // 2, 2, img), ("chip", "core", "img"))
    placed = (P("img", ("chip", "core"), None), P(), P(), P(), P(), P(), P())
    return jax.shard_map(
        on_device,
        mesh=split,
        in_specs=placed,
        out_specs=P(("chip", "core", "img"), None, None, None),
        check_vma=False,
    )
```

```python
import math

import jax
import jax.numpy as jnp
from jax import lax
from jax.sharding import PartitionSpec as P
from jax.experimental.layout import Layout, with_layout_constraint

LANES = 128
SPLIT = 8


CTF_SCALE = 20.0
CTF_PHASE = 0.07
MID = lax.Precision.HIGH


def roots(rows, cols, length, factor):
    phase = rows * cols % length
    angle = phase.astype(jnp.float32) * (2.0 * math.pi / length)
    return (jnp.cos(angle) * factor, -jnp.sin(angle) * factor)


def slot_tables(blk_plane, n_dev):
    plane = blk_plane.reshape(n_dev, -1)
    k_dev = plane.shape[1]
    order = lax.iota(jnp.int32, k_dev)
    same = plane[:, :, None] == plane[:, None, :]
    earlier = order[None, None, :] < order[None, :, None]
    rank = jnp.sum((same & earlier).astype(jnp.int32), axis=2)
    return plane, rank


def send_parts(planes, first_plane, meta, box, n_dev):
    blk_plane, blk_row, blk_col, frac_plane, frac_row, defocus = meta
    n_blk = blk_plane.shape[1]
    own, n_rows, width = planes[0].shape
    x = width * len(planes)
    plane_of, rank = slot_tables(blk_plane, n_dev)
    k_dev = plane_of.shape[1]
    t = lax.iota(jnp.int32, own)[:, None, None, None]
    side = lax.iota(jnp.int32, 2)[None, None, :, None]
    u = lax.iota(jnp.int32, 2)[None, None, None, :]
    target = first_plane + t - side
    match = (plane_of[None, :, None, None, :] == target[..., None]) & (
        rank[None, :, None, None, :] == u[..., None]
    )
    valid = jnp.any(match, axis=-1)
    def pick(values):
        table = values.reshape(n_dev, k_dev)[None, :, None, None, :]
        return jnp.sum(jnp.where(match, table, jnp.zeros_like(table)), axis=-1).reshape(-1)

    rows = pick(blk_row)
    cols = pick(blk_col)
    frac_z = pick(frac_plane)
    frac_y = pick(frac_row)[:, None]
    focus = pick(jnp.broadcast_to(defocus[:, None], blk_plane.shape))
    side_f = jnp.broadcast_to(side, (own, n_dev, 2, 2)).reshape(-1)
    valid = valid.reshape(-1)
    lane = lax.iota(jnp.int32, LANES)
    column_x = cols[:, None] * LANES + lane[None, :]
    fold_x = jnp.minimum(column_x, box - column_x).astype(jnp.float32)
    fold_y = jnp.minimum(rows, box - rows).astype(jnp.float32)
    wave_sq = (fold_x * fold_x + (fold_y * fold_y)[:, None]) / float(box * box)
    ctf_value = -jnp.sin(CTF_SCALE * focus[:, None] * wave_sq + CTF_PHASE)
    weight = jnp.where(side_f == 0, 1.0 - frac_z, frac_z)
    weight = jnp.where(valid, weight, 0.0)
    scale = weight[:, None] * ctf_value
    step = int(math.isqrt(n_rows))
    a = lax.iota(jnp.int32, n_rows // step)[None, :]
    b = lax.iota(jnp.int32, step)[None, :]

    def row_roots(r):
        a_re, a_im = roots(r[:, None], a * step, n_rows, 1.0)
        b_re, b_im = roots(r[:, None], b, n_rows, 1.0)
        w_re = a_re[:, :, None] * b_re[:, None, :] - a_im[:, :, None] * b_im[:, None, :]
        w_im = a_re[:, :, None] * b_im[:, None, :] + a_im[:, :, None] * b_re[:, None, :]
        return w_re.reshape(-1, n_rows), w_im.reshape(-1, n_rows)

    lo_re, lo_im = row_roots(rows)
    hi_re, hi_im = row_roots(rows + 1)
    norm = 1.0 / math.sqrt(n_rows)
    w_re = ((1.0 - frac_y) * lo_re + frac_y * hi_re) * norm
    w_im = ((1.0 - frac_y) * lo_im + frac_y * hi_im) * norm
    n_s = w_re.shape[0] // own
    w_all = jnp.stack([w_re.reshape(own, n_s, n_rows), w_im.reshape(own, n_s, n_rows)], axis=1)
    m = x // SPLIT
    step_n2 = m // len(planes)
    idx = lax.iota(jnp.int32, m)
    c_re, c_im = roots(idx[:, None], idx[None, :], m, 1.0 / math.sqrt(x))
    w_col = jnp.stack(
        [jnp.stack([c_re, -c_im], axis=1), jnp.stack([c_im, c_re], axis=1)], axis=0
    )
    y = None
    for j, piece in enumerate(planes):
        r_t = jnp.einsum("trc,tpsr->tpcs", piece, w_all, precision=MID)
        r_t = with_layout_constraint(r_t, Layout(major_to_minor=(0, 1, 2, 3)))
        r5 = r_t.reshape(own, 2, step_n2, SPLIT, n_s)
        w_j = w_col[:, :, :, j * step_n2:(j + 1) * step_n2]
        y_j = jnp.einsum("qkpn,tpnjs->tqkjs", w_j, r5, precision=MID)
        y = y_j if y is None else y + y_j
    y_re = y[:, 0]
    y_im = y[:, 1]
    n1 = lax.iota(jnp.int32, SPLIT)
    cols_t = cols.reshape(own, n_s)
    e_re, e_im = roots(n1[None, :, None], cols_t[:, None, :], SPLIT, 1.0)
    t_re, t_im = roots(lane[:, None], n1[None, :], box, 1.0)
    e_re = e_re[:, None]
    e_im = e_im[:, None]
    t_re = t_re[None, :, :, None]
    t_im = t_im[None, :, :, None]
    g_re = e_re * t_re - e_im * t_im
    g_im = e_re * t_im + e_im * t_re
    o_re = jnp.sum(g_re * y_re - g_im * y_im, axis=2)
    o_im = jnp.sum(g_re * y_im + g_im * y_re, axis=2)
    o_re = jnp.swapaxes(o_re, 1, 2).reshape(own * n_s, LANES)
    o_im = jnp.swapaxes(o_im, 1, 2).reshape(own * n_s, LANES)
    parts = jnp.stack([scale * o_re, scale * o_im], axis=1)
    parts = parts.reshape(own, n_dev, 4, 2, LANES)
    return jnp.swapaxes(parts, 0, 1).reshape(n_dev, own * 4, 2, LANES)


def gather_parts(recv, blk_plane, me, own, n_slab, n_img):
    n_dev = n_slab * n_img
    plane, rank = slot_tables(blk_plane, n_dev)
    mine = plane[me]
    my_rank = rank[me]
    slots = own * 4

    def place(q, side):
        holder = q // own
        src = (holder % n_slab) * n_img + holder // n_slab
        return src * slots + (q % own) * 4 + side * 2 + my_rank

    flat = recv.reshape(-1, 2 * LANES)
    rows = lax.iota(jnp.int32, flat.shape[0])[None, :]
    pick = (rows == place(mine, 0)[:, None]).astype(jnp.float32) + (
        rows == place(mine + 1, 1)[:, None]
    ).astype(jnp.float32)
    return jnp.dot(pick, flat, precision=lax.Precision.HIGHEST).reshape(-1, 2, LANES)


def on_device(volume, blk_plane, blk_row, blk_col, frac_plane, frac_row, defocus):
    box = volume.shape[2]
    n_slab = lax.axis_size("slab")
    n_img = lax.axis_size("img")
    n_dev = n_slab * n_img
    planes = [lax.all_to_all(volume, "slab", split_axis=0, concat_axis=1, tiled=True)]
    own = planes[0].shape[0]
    first_plane = (lax.axis_index("img") * n_slab + lax.axis_index("slab")) * own
    meta = (blk_plane, blk_row, blk_col, frac_plane, frac_row, defocus)
    parts = send_parts(planes, first_plane, meta, box, n_dev)
    recv = lax.all_to_all(parts, ("slab", "img"), split_axis=0, concat_axis=0, tiled=True)
    me = lax.axis_index("slab") * n_img + lax.axis_index("img")
    total = gather_parts(recv, blk_plane, me, own, n_slab, n_img)
    n_blk = blk_plane.shape[1]
    return total.reshape(-1, n_blk, 2, LANES)


def solution(mesh):
    placed = (P("img", "slab", None), P(), P(), P(), P(), P(), P())
    return jax.shard_map(
        on_device,
        mesh=mesh,
        in_specs=placed,
        out_specs=P(("slab", "img"), None, None, None),
        check_vma=False,
    )
```

```python
import math

import jax
import jax.numpy as jnp
from jax import lax
from jax.sharding import PartitionSpec as P
from jax.experimental.layout import Layout, with_layout_constraint

LANES = 128
SPLIT = 8


CTF_SCALE = 20.0
CTF_PHASE = 0.07
MID = lax.Precision.HIGH


def roots(rows, cols, length, factor):
    phase = rows * cols % length
    angle = phase.astype(jnp.float32) * (2.0 * math.pi / length)
    return (jnp.cos(angle) * factor, -jnp.sin(angle) * factor)


def slot_tables(blk_plane, n_dev):
    plane = blk_plane.reshape(n_dev, -1)
    k_dev = plane.shape[1]
    order = lax.iota(jnp.int32, k_dev)
    same = plane[:, :, None] == plane[:, None, :]
    earlier = order[None, None, :] < order[None, :, None]
    rank = jnp.sum((same & earlier).astype(jnp.int32), axis=2)
    return plane, rank


def send_parts(planes, first_plane, meta, box, n_dev):
    blk_plane, blk_row, blk_col, frac_plane, frac_row, defocus = meta
    n_blk = blk_plane.shape[1]
    own, n_rows, width = planes[0].shape
    x = width * len(planes)
    plane_of, rank = slot_tables(blk_plane, n_dev)
    k_dev = plane_of.shape[1]
    t = lax.iota(jnp.int32, own)[:, None, None, None]
    side = lax.iota(jnp.int32, 2)[None, None, :, None]
    u = lax.iota(jnp.int32, 2)[None, None, None, :]
    target = first_plane + t - side
    match = (plane_of[None, :, None, None, :] == target[..., None]) & (
        rank[None, :, None, None, :] == u[..., None]
    )
    valid = jnp.any(match, axis=-1)
    def pick(values):
        table = values.reshape(n_dev, k_dev)[None, :, None, None, :]
        return jnp.sum(jnp.where(match, table, jnp.zeros_like(table)), axis=-1).reshape(-1)

    rows = pick(blk_row)
    cols = pick(blk_col)
    frac_z = pick(frac_plane)
    frac_y = pick(frac_row)[:, None]
    focus = pick(jnp.broadcast_to(defocus[:, None], blk_plane.shape))
    side_f = jnp.broadcast_to(side, (own, n_dev, 2, 2)).reshape(-1)
    valid = valid.reshape(-1)
    lane = lax.iota(jnp.int32, LANES)
    column_x = cols[:, None] * LANES + lane[None, :]
    fold_x = jnp.minimum(column_x, box - column_x).astype(jnp.float32)
    fold_y = jnp.minimum(rows, box - rows).astype(jnp.float32)
    wave_sq = (fold_x * fold_x + (fold_y * fold_y)[:, None]) / float(box * box)
    ctf_value = -jnp.sin(CTF_SCALE * focus[:, None] * wave_sq + CTF_PHASE)
    weight = jnp.where(side_f == 0, 1.0 - frac_z, frac_z)
    weight = jnp.where(valid, weight, 0.0)
    scale = weight[:, None] * ctf_value
    step = int(math.isqrt(n_rows))
    a = lax.iota(jnp.int32, n_rows // step)[None, :]
    b = lax.iota(jnp.int32, step)[None, :]

    def row_roots(r):
        a_re, a_im = roots(r[:, None], a * step, n_rows, 1.0)
        b_re, b_im = roots(r[:, None], b, n_rows, 1.0)
        w_re = a_re[:, :, None] * b_re[:, None, :] - a_im[:, :, None] * b_im[:, None, :]
        w_im = a_re[:, :, None] * b_im[:, None, :] + a_im[:, :, None] * b_re[:, None, :]
        return w_re.reshape(-1, n_rows), w_im.reshape(-1, n_rows)

    lo_re, lo_im = row_roots(rows)
    hi_re, hi_im = row_roots(rows + 1)
    norm = 1.0 / math.sqrt(n_rows)
    w_re = ((1.0 - frac_y) * lo_re + frac_y * hi_re) * norm
    w_im = ((1.0 - frac_y) * lo_im + frac_y * hi_im) * norm
    n_s = w_re.shape[0] // own
    w_all = jnp.stack([w_re.reshape(own, n_s, n_rows), w_im.reshape(own, n_s, n_rows)], axis=1)
    m = x // SPLIT
    step_n2 = m // len(planes)
    idx = lax.iota(jnp.int32, m)
    c_re, c_im = roots(idx[:, None], idx[None, :], m, 1.0 / math.sqrt(x))
    w_col = jnp.stack(
        [jnp.stack([c_re, -c_im], axis=1), jnp.stack([c_im, c_re], axis=1)], axis=0
    )
    y = None
    for j, piece in enumerate(planes):
        r_t = jnp.einsum("trc,tpsr->tpcs", piece, w_all, precision=MID)
        r_t = with_layout_constraint(r_t, Layout(major_to_minor=(0, 1, 2, 3)))
        r5 = r_t.reshape(own, 2, step_n2, SPLIT, n_s)
        w_j = w_col[:, :, :, j * step_n2:(j + 1) * step_n2]
        y_j = jnp.einsum("qkpn,tpnjs->tqkjs", w_j, r5, precision=MID)
        y = y_j if y is None else y + y_j
    y_re = y[:, 0]
    y_im = y[:, 1]
    n1 = lax.iota(jnp.int32, SPLIT)
    cols_t = cols.reshape(own, n_s)
    e_re, e_im = roots(n1[None, :, None], cols_t[:, None, :], SPLIT, 1.0)
    t_re, t_im = roots(lane[:, None], n1[None, :], box, 1.0)
    e_re = e_re[:, None]
    e_im = e_im[:, None]
    t_re = t_re[None, :, :, None]
    t_im = t_im[None, :, :, None]
    g_re = e_re * t_re - e_im * t_im
    g_im = e_re * t_im + e_im * t_re
    o_re = jnp.sum(g_re * y_re - g_im * y_im, axis=2)
    o_im = jnp.sum(g_re * y_im + g_im * y_re, axis=2)
    o_re = jnp.swapaxes(o_re, 1, 2).reshape(own * n_s, LANES)
    o_im = jnp.swapaxes(o_im, 1, 2).reshape(own * n_s, LANES)
    parts = jnp.stack([scale * o_re, scale * o_im], axis=1)
    parts = parts.reshape(own, n_dev, 4, 2, LANES)
    return jnp.swapaxes(parts, 0, 1).reshape(n_dev, own * 4, 2, LANES)


def gather_parts(recv, blk_plane, me, own, n_slab, n_img):
    n_dev = n_slab * n_img
    plane, rank = slot_tables(blk_plane, n_dev)
    mine = plane[me]
    my_rank = rank[me]
    slots = own * 4

    def place(q, side):
        holder = q // own
        src = holder
        return src * slots + (q % own) * 4 + side * 2 + my_rank

    flat = recv.reshape(-1, 2, LANES)
    return flat[place(mine, 0)] + flat[place(mine + 1, 1)]


def on_device(volume, blk_plane, blk_row, blk_col, frac_plane, frac_row, defocus):
    box = volume.shape[2]
    n_slab = lax.axis_size("slab")
    n_img = lax.axis_size("img")
    n_dev = n_slab * n_img
    planes = [lax.all_to_all(volume, "slab", split_axis=0, concat_axis=1, tiled=True)]
    own = planes[0].shape[0]
    first_plane = (lax.axis_index("img") * n_slab + lax.axis_index("slab")) * own
    meta = (blk_plane, blk_row, blk_col, frac_plane, frac_row, defocus)
    parts = send_parts(planes, first_plane, meta, box, n_dev)
    parts = jnp.swapaxes(parts.reshape(n_slab, n_img, *parts.shape[1:]), 0, 1)
    parts = parts.reshape(n_dev, *parts.shape[2:])
    recv = lax.all_to_all(parts, ("img", "slab"), split_axis=0, concat_axis=0, tiled=True)
    me = lax.axis_index("slab") * n_img + lax.axis_index("img")
    total = gather_parts(recv, blk_plane, me, own, n_slab, n_img)
    n_blk = blk_plane.shape[1]
    return total.reshape(-1, n_blk, 2, LANES)


def solution(mesh):
    placed = (P("img", "slab", None), P(), P(), P(), P(), P(), P())
    return jax.shard_map(
        on_device,
        mesh=mesh,
        in_specs=placed,
        out_specs=P(("slab", "img"), None, None, None),
        check_vma=False,
    )
```

```python
import math

import jax
import jax.numpy as jnp
from jax import lax
from jax.sharding import PartitionSpec as P
from jax.experimental.layout import Layout, with_layout_constraint

LANES = 128
SPLIT = 8


CTF_SCALE = 20.0
CTF_PHASE = 0.07
MID = lax.Precision.HIGH


def roots(rows, cols, length, factor):
    phase = rows * cols % length
    angle = phase.astype(jnp.float32) * (2.0 * math.pi / length)
    return (jnp.cos(angle) * factor, -jnp.sin(angle) * factor)


def slot_tables(blk_plane, n_dev):
    plane = blk_plane.reshape(n_dev, -1)
    k_dev = plane.shape[1]
    order = lax.iota(jnp.int32, k_dev)
    same = plane[:, :, None] == plane[:, None, :]
    earlier = order[None, None, :] < order[None, :, None]
    rank = jnp.sum((same & earlier).astype(jnp.int32), axis=2)
    return plane, rank


def send_parts(planes, first_plane, meta, box, n_dev):
    blk_plane, blk_row, blk_col, frac_plane, frac_row, defocus = meta
    n_blk = blk_plane.shape[1]
    own, n_rows, width = planes[0].shape
    x = width * len(planes)
    plane_of, rank = slot_tables(blk_plane, n_dev)
    k_dev = plane_of.shape[1]
    t = lax.iota(jnp.int32, own)[:, None, None, None]
    side = lax.iota(jnp.int32, 2)[None, None, :, None]
    u = lax.iota(jnp.int32, 2)[None, None, None, :]
    target = first_plane + t - side
    match = (plane_of[None, :, None, None, :] == target[..., None]) & (
        rank[None, :, None, None, :] == u[..., None]
    )
    valid = jnp.any(match, axis=-1)
    def pick(values):
        table = values.reshape(n_dev, k_dev)[None, :, None, None, :]
        return jnp.sum(jnp.where(match, table, jnp.zeros_like(table)), axis=-1).reshape(-1)

    rows = pick(blk_row)
    cols = pick(blk_col)
    frac_z = pick(frac_plane)
    frac_y = pick(frac_row)[:, None]
    focus = pick(jnp.broadcast_to(defocus[:, None], blk_plane.shape))
    side_f = jnp.broadcast_to(side, (own, n_dev, 2, 2)).reshape(-1)
    valid = valid.reshape(-1)
    lane = lax.iota(jnp.int32, LANES)
    column_x = cols[:, None] * LANES + lane[None, :]
    fold_x = jnp.minimum(column_x, box - column_x).astype(jnp.float32)
    fold_y = jnp.minimum(rows, box - rows).astype(jnp.float32)
    wave_sq = (fold_x * fold_x + (fold_y * fold_y)[:, None]) / float(box * box)
    ctf_value = -jnp.sin(CTF_SCALE * focus[:, None] * wave_sq + CTF_PHASE)
    weight = jnp.where(side_f == 0, 1.0 - frac_z, frac_z)
    weight = jnp.where(valid, weight, 0.0)
    scale = weight[:, None] * ctf_value
    step = int(math.isqrt(n_rows))
    a = lax.iota(jnp.int32, n_rows // step)[None, :]
    b = lax.iota(jnp.int32, step)[None, :]

    def row_roots(r):
        a_re, a_im = roots(r[:, None], a * step, n_rows, 1.0)
        b_re, b_im = roots(r[:, None], b, n_rows, 1.0)
        w_re = a_re[:, :, None] * b_re[:, None, :] - a_im[:, :, None] * b_im[:, None, :]
        w_im = a_re[:, :, None] * b_im[:, None, :] + a_im[:, :, None] * b_re[:, None, :]
        return w_re.reshape(-1, n_rows), w_im.reshape(-1, n_rows)

    lo_re, lo_im = row_roots(rows)
    hi_re, hi_im = row_roots(rows + 1)
    norm = 1.0 / math.sqrt(n_rows)
    w_re = ((1.0 - frac_y) * lo_re + frac_y * hi_re) * norm
    w_im = ((1.0 - frac_y) * lo_im + frac_y * hi_im) * norm
    n_s = w_re.shape[0] // own
    w_all = jnp.stack([w_re.reshape(own, n_s, n_rows), w_im.reshape(own, n_s, n_rows)], axis=1)
    m = x // SPLIT
    step_n2 = m // len(planes)
    idx = lax.iota(jnp.int32, m)
    c_re, c_im = roots(idx[:, None], idx[None, :], m, 1.0 / math.sqrt(x))
    w_col = jnp.stack(
        [jnp.stack([c_re, -c_im], axis=1), jnp.stack([c_im, c_re], axis=1)], axis=0
    )
    y = None
    for j, piece in enumerate(planes):
        r_t = jnp.einsum("trc,tpsr->tpcs", piece, w_all, precision=MID)
        r_t = with_layout_constraint(r_t, Layout(major_to_minor=(0, 1, 2, 3)))
        r5 = r_t.reshape(own, 2, step_n2, SPLIT, n_s)
        w_j = w_col[:, :, :, j * step_n2:(j + 1) * step_n2]
        y_j = jnp.einsum("qkpn,tpnjs->tqkjs", w_j, r5, precision=MID)
        y = y_j if y is None else y + y_j
    y_re = y[:, 0]
    y_im = y[:, 1]
    n1 = lax.iota(jnp.int32, SPLIT)
    cols_t = cols.reshape(own, n_s)
    e_re, e_im = roots(n1[None, :, None], cols_t[:, None, :], SPLIT, 1.0)
    t_re, t_im = roots(lane[:, None], n1[None, :], box, 1.0)
    e_re = e_re[:, None]
    e_im = e_im[:, None]
    t_re = t_re[None, :, :, None]
    t_im = t_im[None, :, :, None]
    g_re = e_re * t_re - e_im * t_im
    g_im = e_re * t_im + e_im * t_re
    o_re = jnp.sum(g_re * y_re - g_im * y_im, axis=2)
    o_im = jnp.sum(g_re * y_im + g_im * y_re, axis=2)
    o_re = jnp.swapaxes(o_re, 1, 2).reshape(own * n_s, LANES)
    o_im = jnp.swapaxes(o_im, 1, 2).reshape(own * n_s, LANES)
    parts = jnp.stack([scale * o_re, scale * o_im], axis=1)
    parts = parts.reshape(own, n_dev, 4, 2, LANES)
    return jnp.swapaxes(parts, 0, 1).reshape(n_dev, own * 4 * 2, LANES)


def gather_parts(recv, blk_plane, me, own, n_slab, n_img):
    n_dev = n_slab * n_img
    plane, rank = slot_tables(blk_plane, n_dev)
    mine = plane[me]
    my_rank = rank[me]
    slots = own * 4

    def place(q, side):
        holder = q // own
        src = (holder % n_slab) * n_img + holder // n_slab
        return src * slots + (q % own) * 4 + side * 2 + my_rank

    flat = recv.reshape(-1, 2, LANES)
    return flat[place(mine, 0)] + flat[place(mine + 1, 1)]


def on_device(volume, blk_plane, blk_row, blk_col, frac_plane, frac_row, defocus):
    box = volume.shape[2]
    n_slab = lax.axis_size("slab")
    n_img = lax.axis_size("img")
    n_dev = n_slab * n_img
    planes = [lax.all_to_all(volume, "slab", split_axis=0, concat_axis=1, tiled=True)]
    own = planes[0].shape[0]
    first_plane = (lax.axis_index("img") * n_slab + lax.axis_index("slab")) * own
    meta = (blk_plane, blk_row, blk_col, frac_plane, frac_row, defocus)
    parts = send_parts(planes, first_plane, meta, box, n_dev)
    recv = lax.all_to_all(parts, ("slab", "img"), split_axis=0, concat_axis=0, tiled=True)
    me = lax.axis_index("slab") * n_img + lax.axis_index("img")
    total = gather_parts(recv, blk_plane, me, own, n_slab, n_img)
    n_blk = blk_plane.shape[1]
    return total.reshape(-1, n_blk, 2, LANES)


def solution(mesh):
    placed = (P("img", "slab", None), P(), P(), P(), P(), P(), P())
    return jax.shard_map(
        on_device,
        mesh=mesh,
        in_specs=placed,
        out_specs=P(("slab", "img"), None, None, None),
        check_vma=False,
    )
```

```python
import math

import jax
import jax.numpy as jnp
from jax import lax
from jax.sharding import PartitionSpec as P
from jax.experimental.layout import Layout, with_layout_constraint

LANES = 128
SPLIT = 8


CTF_SCALE = 20.0
CTF_PHASE = 0.07
MID = lax.Precision.HIGH


def roots(rows, cols, length, factor):
    phase = rows * cols % length
    angle = phase.astype(jnp.float32) * (2.0 * math.pi / length)
    return (jnp.cos(angle) * factor, -jnp.sin(angle) * factor)


def slot_tables(blk_plane, n_dev):
    plane = blk_plane.reshape(n_dev, -1)
    k_dev = plane.shape[1]
    order = lax.iota(jnp.int32, k_dev)
    same = plane[:, :, None] == plane[:, None, :]
    earlier = order[None, None, :] < order[None, :, None]
    rank = jnp.sum((same & earlier).astype(jnp.int32), axis=2)
    return plane, rank


def send_parts(planes, first_plane, meta, box, n_dev):
    blk_plane, blk_row, blk_col, frac_plane, frac_row, defocus = meta
    n_blk = blk_plane.shape[1]
    own, n_rows, width = planes[0].shape
    x = width * len(planes)
    plane_of, rank = slot_tables(blk_plane, n_dev)
    k_dev = plane_of.shape[1]
    t = lax.iota(jnp.int32, own)[:, None, None, None]
    side = lax.iota(jnp.int32, 2)[None, None, :, None]
    u = lax.iota(jnp.int32, 2)[None, None, None, :]
    target = first_plane + t - side
    match = (plane_of[None, :, None, None, :] == target[..., None]) & (
        rank[None, :, None, None, :] == u[..., None]
    )
    valid = jnp.any(match, axis=-1)
    def pick(values):
        table = values.reshape(n_dev, k_dev)[None, :, None, None, :]
        return jnp.sum(jnp.where(match, table, jnp.zeros_like(table)), axis=-1).reshape(-1)

    rows = pick(blk_row)
    cols = pick(blk_col)
    frac_z = pick(frac_plane)
    frac_y = pick(frac_row)[:, None]
    focus = pick(jnp.broadcast_to(defocus[:, None], blk_plane.shape))
    side_f = jnp.broadcast_to(side, (own, n_dev, 2, 2)).reshape(-1)
    valid = valid.reshape(-1)
    lane = lax.iota(jnp.int32, LANES)
    column_x = cols[:, None] * LANES + lane[None, :]
    fold_x = jnp.minimum(column_x, box - column_x).astype(jnp.float32)
    fold_y = jnp.minimum(rows, box - rows).astype(jnp.float32)
    wave_sq = (fold_x * fold_x + (fold_y * fold_y)[:, None]) / float(box * box)
    ctf_value = -jnp.sin(CTF_SCALE * focus[:, None] * wave_sq + CTF_PHASE)
    weight = jnp.where(side_f == 0, 1.0 - frac_z, frac_z)
    weight = jnp.where(valid, weight, 0.0)
    scale = weight[:, None] * ctf_value
    step = int(math.isqrt(n_rows))
    a = lax.iota(jnp.int32, n_rows // step)[None, :]
    b = lax.iota(jnp.int32, step)[None, :]

    def row_roots(r):
        a_re, a_im = roots(r[:, None], a * step, n_rows, 1.0)
        b_re, b_im = roots(r[:, None], b, n_rows, 1.0)
        w_re = a_re[:, :, None] * b_re[:, None, :] - a_im[:, :, None] * b_im[:, None, :]
        w_im = a_re[:, :, None] * b_im[:, None, :] + a_im[:, :, None] * b_re[:, None, :]
        return w_re.reshape(-1, n_rows), w_im.reshape(-1, n_rows)

    lo_re, lo_im = row_roots(rows)
    hi_re, hi_im = row_roots(rows + 1)
    norm = 1.0 / math.sqrt(n_rows)
    w_re = ((1.0 - frac_y) * lo_re + frac_y * hi_re) * norm
    w_im = ((1.0 - frac_y) * lo_im + frac_y * hi_im) * norm
    n_s = w_re.shape[0] // own
    w_all = jnp.stack([w_re.reshape(own, n_s, n_rows), w_im.reshape(own, n_s, n_rows)], axis=1)
    m = x // SPLIT
    step_n2 = m // len(planes)
    idx = lax.iota(jnp.int32, m)
    c_re, c_im = roots(idx[:, None], idx[None, :], m, 1.0 / math.sqrt(x))
    w_col = jnp.stack(
        [jnp.stack([c_re, -c_im], axis=1), jnp.stack([c_im, c_re], axis=1)], axis=0
    )
    y = None
    for j, piece in enumerate(planes):
        r_t = jnp.einsum("trc,tpsr->tpcs", piece, w_all, precision=MID)
        r_t = with_layout_constraint(r_t, Layout(major_to_minor=(0, 1, 2, 3)))
        r5 = r_t.reshape(own, 2, step_n2, SPLIT, n_s)
        w_j = w_col[:, :, :, j * step_n2:(j + 1) * step_n2]
        y_j = jnp.einsum("qkpn,tpnjs->tqkjs", w_j, r5, precision=MID)
        y = y_j if y is None else y + y_j
    y_re = y[:, 0]
    y_im = y[:, 1]
    n1 = lax.iota(jnp.int32, SPLIT)
    cols_t = cols.reshape(own, n_s)
    e_re, e_im = roots(n1[None, :, None], cols_t[:, None, :], SPLIT, 1.0)
    t_re, t_im = roots(lane[:, None], n1[None, :], box, 1.0)
    e_re = e_re[:, None]
    e_im = e_im[:, None]
    t_re = t_re[None, :, :, None]
    t_im = t_im[None, :, :, None]
    g_re = e_re * t_re - e_im * t_im
    g_im = e_re * t_im + e_im * t_re
    o_re = jnp.sum(g_re * y_re - g_im * y_im, axis=2)
    o_im = jnp.sum(g_re * y_im + g_im * y_re, axis=2)
    o_re = jnp.swapaxes(o_re, 1, 2).reshape(own * n_s, LANES)
    o_im = jnp.swapaxes(o_im, 1, 2).reshape(own * n_s, LANES)
    parts = jnp.stack([scale * o_re, scale * o_im], axis=1)
    parts = parts.reshape(own, n_dev, 4, 2, LANES)
    return jnp.swapaxes(parts, 0, 1).reshape(n_dev, own * 4 * 2, LANES)


def gather_parts(recv, blk_plane, me, own, n_slab, n_img):
    n_dev = n_slab * n_img
    plane, rank = slot_tables(blk_plane, n_dev)
    mine = plane[me]
    my_rank = rank[me]
    slots = own * 4

    def place(q, side):
        holder = q // own
        src = (holder % n_slab) * n_img + holder // n_slab
        return src * slots + (q % own) * 4 + side * 2 + my_rank

    flat = recv.reshape(-1, 2, LANES)
    rows = lax.iota(jnp.int32, flat.shape[0])[None, :]
    pick = (rows == place(mine, 0)[:, None]).astype(jnp.float32) + (
        rows == place(mine + 1, 1)[:, None]
    ).astype(jnp.float32)
    return jnp.einsum("kj,jpl->kpl", pick, flat, precision=lax.Precision.HIGHEST)


def on_device(volume, blk_plane, blk_row, blk_col, frac_plane, frac_row, defocus):
    box = volume.shape[2]
    n_slab = lax.axis_size("slab")
    n_img = lax.axis_size("img")
    n_dev = n_slab * n_img
    planes = [lax.all_to_all(volume, "slab", split_axis=0, concat_axis=1, tiled=True)]
    own = planes[0].shape[0]
    first_plane = (lax.axis_index("img") * n_slab + lax.axis_index("slab")) * own
    meta = (blk_plane, blk_row, blk_col, frac_plane, frac_row, defocus)
    parts = send_parts(planes, first_plane, meta, box, n_dev)
    recv = lax.all_to_all(parts, ("slab", "img"), split_axis=0, concat_axis=0, tiled=True)
    me = lax.axis_index("slab") * n_img + lax.axis_index("img")
    total = gather_parts(recv, blk_plane, me, own, n_slab, n_img)
    n_blk = blk_plane.shape[1]
    return total.reshape(-1, n_blk, 2, LANES)


def solution(mesh):
    placed = (P("img", "slab", None), P(), P(), P(), P(), P(), P())
    return jax.shard_map(
        on_device,
        mesh=mesh,
        in_specs=placed,
        out_specs=P(("slab", "img"), None, None, None),
        check_vma=False,
    )
```

```python
import math

import jax
import jax.numpy as jnp
from jax import lax
from jax.sharding import PartitionSpec as P
from jax.experimental.layout import Layout, with_layout_constraint

LANES = 128
SPLIT = 8


CTF_SCALE = 20.0
CTF_PHASE = 0.07
MID = lax.Precision.HIGH


def roots(rows, cols, length, factor):
    phase = rows * cols % length
    angle = phase.astype(jnp.float32) * (2.0 * math.pi / length)
    return (jnp.cos(angle) * factor, -jnp.sin(angle) * factor)


def slot_tables(blk_plane, n_dev):
    plane = blk_plane.reshape(n_dev, -1)
    k_dev = plane.shape[1]
    order = lax.iota(jnp.int32, k_dev)
    same = plane[:, :, None] == plane[:, None, :]
    earlier = order[None, None, :] < order[None, :, None]
    rank = jnp.sum((same & earlier).astype(jnp.int32), axis=2)
    return plane, rank


def send_parts(planes, first_plane, meta, box, n_dev):
    blk_plane, blk_row, blk_col, frac_plane, frac_row, defocus = meta
    n_blk = blk_plane.shape[1]
    own, n_rows, width = planes[0].shape
    x = width * len(planes)
    plane_of, rank = slot_tables(blk_plane, n_dev)
    k_dev = plane_of.shape[1]
    t = lax.iota(jnp.int32, own)[:, None, None, None]
    side = lax.iota(jnp.int32, 2)[None, None, :, None]
    u = lax.iota(jnp.int32, 2)[None, None, None, :]
    target = first_plane + t - side
    match = (plane_of[None, :, None, None, :] == target[..., None]) & (
        rank[None, :, None, None, :] == u[..., None]
    )
    valid = jnp.any(match, axis=-1)
    def pick(values):
        table = values.reshape(n_dev, k_dev)[None, :, None, None, :]
        return jnp.sum(jnp.where(match, table, jnp.zeros_like(table)), axis=-1).reshape(-1)

    rows = pick(blk_row)
    cols = pick(blk_col)
    frac_z = pick(frac_plane)
    frac_y = pick(frac_row)[:, None]
    focus = pick(jnp.broadcast_to(defocus[:, None], blk_plane.shape))
    side_f = jnp.broadcast_to(side, (own, n_dev, 2, 2)).reshape(-1)
    valid = valid.reshape(-1)
    lane = lax.iota(jnp.int32, LANES)
    column_x = cols[:, None] * LANES + lane[None, :]
    fold_x = jnp.minimum(column_x, box - column_x).astype(jnp.float32)
    fold_y = jnp.minimum(rows, box - rows).astype(jnp.float32)
    wave_sq = (fold_x * fold_x + (fold_y * fold_y)[:, None]) / float(box * box)
    ctf_value = -jnp.sin(CTF_SCALE * focus[:, None] * wave_sq + CTF_PHASE)
    weight = jnp.where(side_f == 0, 1.0 - frac_z, frac_z)
    weight = jnp.where(valid, weight, 0.0)
    scale = weight[:, None] * ctf_value
    step = int(math.isqrt(n_rows))
    a = lax.iota(jnp.int32, n_rows // step)[None, :]
    b = lax.iota(jnp.int32, step)[None, :]

    def row_roots(r):
        a_re, a_im = roots(r[:, None], a * step, n_rows, 1.0)
        b_re, b_im = roots(r[:, None], b, n_rows, 1.0)
        w_re = a_re[:, :, None] * b_re[:, None, :] - a_im[:, :, None] * b_im[:, None, :]
        w_im = a_re[:, :, None] * b_im[:, None, :] + a_im[:, :, None] * b_re[:, None, :]
        return w_re.reshape(-1, n_rows), w_im.reshape(-1, n_rows)

    lo_re, lo_im = row_roots(rows)
    hi_re, hi_im = row_roots(rows + 1)
    norm = 1.0 / math.sqrt(n_rows)
    w_re = ((1.0 - frac_y) * lo_re + frac_y * hi_re) * norm
    w_im = ((1.0 - frac_y) * lo_im + frac_y * hi_im) * norm
    n_s = w_re.shape[0] // own
    w_all = jnp.stack([w_re.reshape(own, n_s, n_rows), w_im.reshape(own, n_s, n_rows)], axis=1)
    m = x // SPLIT
    step_n2 = m // len(planes)
    idx = lax.iota(jnp.int32, m)
    c_re, c_im = roots(idx[:, None], idx[None, :], m, 1.0 / math.sqrt(x))
    w_col = jnp.stack(
        [jnp.stack([c_re, -c_im], axis=1), jnp.stack([c_im, c_re], axis=1)], axis=0
    )
    y = None
    for j, piece in enumerate(planes):
        r_t = jnp.einsum("trc,tpsr->tpcs", piece, w_all, precision=MID)
        r_t = with_layout_constraint(r_t, Layout(major_to_minor=(0, 1, 2, 3)))
        r5 = r_t.reshape(own, 2, step_n2, SPLIT, n_s)
        w_j = w_col[:, :, :, j * step_n2:(j + 1) * step_n2]
        y_j = jnp.einsum("qkpn,tpnjs->tqkjs", w_j, r5, precision=MID)
        y = y_j if y is None else y + y_j
    y_re = y[:, 0]
    y_im = y[:, 1]
    n1 = lax.iota(jnp.int32, SPLIT)
    cols_t = cols.reshape(own, n_s)
    e_re, e_im = roots(n1[None, :, None], cols_t[:, None, :], SPLIT, 1.0)
    t_re, t_im = roots(lane[:, None], n1[None, :], box, 1.0)
    e_re = e_re[:, None]
    e_im = e_im[:, None]
    t_re = t_re[None, :, :, None]
    t_im = t_im[None, :, :, None]
    g_re = e_re * t_re - e_im * t_im
    g_im = e_re * t_im + e_im * t_re
    o_re = jnp.sum(g_re * y_re - g_im * y_im, axis=2)
    o_im = jnp.sum(g_re * y_im + g_im * y_re, axis=2)
    o_re = jnp.swapaxes(o_re, 1, 2).reshape(own * n_s, LANES)
    o_im = jnp.swapaxes(o_im, 1, 2).reshape(own * n_s, LANES)
    p_re = jnp.swapaxes((scale * o_re).reshape(own, n_dev, 4, LANES), 0, 1)
    p_im = jnp.swapaxes((scale * o_im).reshape(own, n_dev, 4, LANES), 0, 1)
    return jnp.concatenate(
        [p_re.reshape(n_dev, own * 4, LANES), p_im.reshape(n_dev, own * 4, LANES)], axis=1
    )


def gather_parts(recv, blk_plane, me, own, n_slab, n_img):
    n_dev = n_slab * n_img
    plane, rank = slot_tables(blk_plane, n_dev)
    mine = plane[me]
    my_rank = rank[me]
    slots = own * 4

    def place(q, side):
        holder = q // own
        src = (holder % n_slab) * n_img + holder // n_slab
        return src * slots + (q % own) * 4 + side * 2 + my_rank

    n_src = recv.shape[0]
    split = recv.reshape(n_src, 2, slots, LANES)
    rows = lax.iota(jnp.int32, n_src * slots)[None, :]
    pick = (rows == place(mine, 0)[:, None]).astype(jnp.float32) + (
        rows == place(mine + 1, 1)[:, None]
    ).astype(jnp.float32)
    pick = pick.reshape(-1, n_src, slots)
    return jnp.einsum("kas,apsl->kpl", pick, split, precision=lax.Precision.HIGHEST)


def on_device(volume, blk_plane, blk_row, blk_col, frac_plane, frac_row, defocus):
    box = volume.shape[2]
    n_slab = lax.axis_size("slab")
    n_img = lax.axis_size("img")
    n_dev = n_slab * n_img
    planes = [lax.all_to_all(volume, "slab", split_axis=0, concat_axis=1, tiled=True)]
    own = planes[0].shape[0]
    first_plane = (lax.axis_index("img") * n_slab + lax.axis_index("slab")) * own
    meta = (blk_plane, blk_row, blk_col, frac_plane, frac_row, defocus)
    parts = send_parts(planes, first_plane, meta, box, n_dev)
    recv = lax.all_to_all(parts, ("slab", "img"), split_axis=0, concat_axis=0, tiled=True)
    me = lax.axis_index("slab") * n_img + lax.axis_index("img")
    total = gather_parts(recv, blk_plane, me, own, n_slab, n_img)
    n_blk = blk_plane.shape[1]
    return total.reshape(-1, n_blk, 2, LANES)


def solution(mesh):
    placed = (P("img", "slab", None), P(), P(), P(), P(), P(), P())
    return jax.shard_map(
        on_device,
        mesh=mesh,
        in_specs=placed,
        out_specs=P(("slab", "img"), None, None, None),
        check_vma=False,
    )
```

```python
import math

import jax
import jax.numpy as jnp
from jax import lax
from jax.sharding import PartitionSpec as P
from jax.experimental.layout import Layout, with_layout_constraint

LANES = 128
SPLIT = 8


CTF_SCALE = 20.0
CTF_PHASE = 0.07
MID = lax.Precision.HIGH


def roots(rows, cols, length, factor):
    phase = rows * cols % length
    angle = phase.astype(jnp.float32) * (2.0 * math.pi / length)
    return (jnp.cos(angle) * factor, -jnp.sin(angle) * factor)


def slot_tables(blk_plane, n_dev):
    plane = blk_plane.reshape(n_dev, -1)
    k_dev = plane.shape[1]
    order = lax.iota(jnp.int32, k_dev)
    same = plane[:, :, None] == plane[:, None, :]
    earlier = order[None, None, :] < order[None, :, None]
    rank = jnp.sum((same & earlier).astype(jnp.int32), axis=2)
    return plane, rank


def send_parts(planes, first_plane, meta, box, n_dev):
    blk_plane, blk_row, blk_col, frac_plane, frac_row, defocus = meta
    n_blk = blk_plane.shape[1]
    own, n_rows, width = planes[0].shape
    x = width * len(planes)
    plane_of, rank = slot_tables(blk_plane, n_dev)
    k_dev = plane_of.shape[1]
    t = lax.iota(jnp.int32, own)[:, None, None, None]
    side = lax.iota(jnp.int32, 2)[None, None, :, None]
    u = lax.iota(jnp.int32, 2)[None, None, None, :]
    target = first_plane + t - side
    match = (plane_of[None, :, None, None, :] == target[..., None]) & (
        rank[None, :, None, None, :] == u[..., None]
    )
    valid = jnp.any(match, axis=-1)
    def pick(values):
        table = values.reshape(n_dev, k_dev)[None, :, None, None, :]
        return jnp.sum(jnp.where(match, table, jnp.zeros_like(table)), axis=-1).reshape(-1)

    rows = pick(blk_row)
    cols = pick(blk_col)
    frac_z = pick(frac_plane)
    frac_y = pick(frac_row)[:, None]
    focus = pick(jnp.broadcast_to(defocus[:, None], blk_plane.shape))
    side_f = jnp.broadcast_to(side, (own, n_dev, 2, 2)).reshape(-1)
    valid = valid.reshape(-1)
    lane = lax.iota(jnp.int32, LANES)
    column_x = cols[:, None] * LANES + lane[None, :]
    fold_x = jnp.minimum(column_x, box - column_x).astype(jnp.float32)
    fold_y = jnp.minimum(rows, box - rows).astype(jnp.float32)
    wave_sq = (fold_x * fold_x + (fold_y * fold_y)[:, None]) / float(box * box)
    ctf_value = -jnp.sin(CTF_SCALE * focus[:, None] * wave_sq + CTF_PHASE)
    weight = jnp.where(side_f == 0, 1.0 - frac_z, frac_z)
    weight = jnp.where(valid, weight, 0.0)
    scale = weight[:, None] * ctf_value
    step = int(math.isqrt(n_rows))
    a = lax.iota(jnp.int32, n_rows // step)[None, :]
    b = lax.iota(jnp.int32, step)[None, :]

    def row_roots(r):
        a_re, a_im = roots(r[:, None], a * step, n_rows, 1.0)
        b_re, b_im = roots(r[:, None], b, n_rows, 1.0)
        w_re = a_re[:, :, None] * b_re[:, None, :] - a_im[:, :, None] * b_im[:, None, :]
        w_im = a_re[:, :, None] * b_im[:, None, :] + a_im[:, :, None] * b_re[:, None, :]
        return w_re.reshape(-1, n_rows), w_im.reshape(-1, n_rows)

    lo_re, lo_im = row_roots(rows)
    hi_re, hi_im = row_roots(rows + 1)
    norm = 1.0 / math.sqrt(n_rows)
    w_re = ((1.0 - frac_y) * lo_re + frac_y * hi_re) * norm
    w_im = ((1.0 - frac_y) * lo_im + frac_y * hi_im) * norm
    n_s = w_re.shape[0] // own
    w_all = jnp.stack([w_re.reshape(own, n_s, n_rows), w_im.reshape(own, n_s, n_rows)], axis=1)
    m = x // SPLIT
    step_n2 = m // len(planes)
    idx = lax.iota(jnp.int32, m)
    c_re, c_im = roots(idx[:, None], idx[None, :], m, 1.0 / math.sqrt(x))
    w_col = jnp.stack(
        [jnp.stack([c_re, -c_im], axis=1), jnp.stack([c_im, c_re], axis=1)], axis=0
    )
    y = None
    for j, piece in enumerate(planes):
        r_t = jnp.einsum("trc,tpsr->tpcs", piece, w_all, precision=MID)
        r_t = with_layout_constraint(r_t, Layout(major_to_minor=(0, 1, 2, 3)))
        r5 = r_t.reshape(own, 2, step_n2, SPLIT, n_s)
        w_j = w_col[:, :, :, j * step_n2:(j + 1) * step_n2]
        y_j = jnp.einsum("qkpn,tpnjs->tqkjs", w_j, r5, precision=MID)
        y = y_j if y is None else y + y_j
    y_re = y[:, 0]
    y_im = y[:, 1]
    n1 = lax.iota(jnp.int32, SPLIT)
    cols_t = cols.reshape(own, n_s)
    e_re, e_im = roots(n1[None, :, None], cols_t[:, None, :], SPLIT, 1.0)
    t_re, t_im = roots(lane[:, None], n1[None, :], box, 1.0)
    e_re = e_re[:, None]
    e_im = e_im[:, None]
    t_re = t_re[None, :, :, None]
    t_im = t_im[None, :, :, None]
    g_re = e_re * t_re - e_im * t_im
    g_im = e_re * t_im + e_im * t_re
    scale_t = jnp.swapaxes(scale.reshape(own, n_s, LANES), 1, 2)
    o_re = jnp.sum(g_re * y_re - g_im * y_im, axis=2) * scale_t
    o_im = jnp.sum(g_re * y_im + g_im * y_re, axis=2) * scale_t
    o_re = jnp.swapaxes(o_re, 1, 2).reshape(own * n_s, LANES)
    o_im = jnp.swapaxes(o_im, 1, 2).reshape(own * n_s, LANES)
    parts = jnp.stack([o_re, o_im], axis=1)
    parts = parts.reshape(own, n_dev, 4, 2, LANES)
    return jnp.swapaxes(parts, 0, 1).reshape(n_dev, own * 4 * 2, LANES)


def gather_parts(recv, blk_plane, me, own, n_slab, n_img):
    n_dev = n_slab * n_img
    plane, rank = slot_tables(blk_plane, n_dev)
    mine = plane[me]
    my_rank = rank[me]
    slots = own * 4

    def place(q, side):
        holder = q // own
        src = (holder % n_slab) * n_img + holder // n_slab
        return src * slots + (q % own) * 4 + side * 2 + my_rank

    flat = recv.reshape(-1, 2, LANES)
    rows = lax.iota(jnp.int32, flat.shape[0])[None, :]
    pick = (rows == place(mine, 0)[:, None]).astype(jnp.float32) + (
        rows == place(mine + 1, 1)[:, None]
    ).astype(jnp.float32)
    return jnp.einsum("kj,jpl->kpl", pick, flat, precision=lax.Precision.HIGHEST)


def on_device(volume, blk_plane, blk_row, blk_col, frac_plane, frac_row, defocus):
    box = volume.shape[2]
    n_slab = lax.axis_size("slab")
    n_img = lax.axis_size("img")
    n_dev = n_slab * n_img
    planes = [lax.all_to_all(volume, "slab", split_axis=0, concat_axis=1, tiled=True)]
    own = planes[0].shape[0]
    first_plane = (lax.axis_index("img") * n_slab + lax.axis_index("slab")) * own
    meta = (blk_plane, blk_row, blk_col, frac_plane, frac_row, defocus)
    parts = send_parts(planes, first_plane, meta, box, n_dev)
    recv = lax.all_to_all(parts, ("slab", "img"), split_axis=0, concat_axis=0, tiled=True)
    me = lax.axis_index("slab") * n_img + lax.axis_index("img")
    total = gather_parts(recv, blk_plane, me, own, n_slab, n_img)
    n_blk = blk_plane.shape[1]
    return total.reshape(-1, n_blk, 2, LANES)


def solution(mesh):
    placed = (P("img", "slab", None), P(), P(), P(), P(), P(), P())
    return jax.shard_map(
        on_device,
        mesh=mesh,
        in_specs=placed,
        out_specs=P(("slab", "img"), None, None, None),
        check_vma=False,
    )
```

```python
import math

import jax
import jax.numpy as jnp
from jax import lax
from jax.sharding import PartitionSpec as P
from jax.experimental.layout import Layout, with_layout_constraint

LANES = 128
SPLIT = 8


CTF_SCALE = 20.0
CTF_PHASE = 0.07
MID = lax.Precision.HIGH


def roots(rows, cols, length, factor):
    phase = rows * cols % length
    angle = phase.astype(jnp.float32) * (2.0 * math.pi / length)
    return (jnp.cos(angle) * factor, -jnp.sin(angle) * factor)


def slot_tables(blk_plane, n_dev):
    plane = blk_plane.reshape(n_dev, -1)
    k_dev = plane.shape[1]
    order = lax.iota(jnp.int32, k_dev)
    same = plane[:, :, None] == plane[:, None, :]
    earlier = order[None, None, :] < order[None, :, None]
    rank = jnp.sum((same & earlier).astype(jnp.int32), axis=2)
    return plane, rank


def send_parts(planes, first_plane, meta, box, n_dev):
    blk_plane, blk_row, blk_col, frac_plane, frac_row, defocus = meta
    n_blk = blk_plane.shape[1]
    own, n_rows, width = planes[0].shape
    x = width * len(planes)
    plane_of, rank = slot_tables(blk_plane, n_dev)
    k_dev = plane_of.shape[1]
    t = lax.iota(jnp.int32, own)[:, None, None, None]
    side = lax.iota(jnp.int32, 2)[None, None, :, None]
    u = lax.iota(jnp.int32, 2)[None, None, None, :]
    target = first_plane + t - side
    match = (plane_of[None, :, None, None, :] == target[..., None]) & (
        rank[None, :, None, None, :] == u[..., None]
    )
    valid = jnp.any(match, axis=-1)
    def pick(values):
        table = values.reshape(n_dev, k_dev)[None, :, None, None, :]
        return jnp.sum(jnp.where(match, table, jnp.zeros_like(table)), axis=-1).reshape(-1)

    rows = pick(blk_row)
    cols = pick(blk_col)
    frac_z = pick(frac_plane)
    frac_y = pick(frac_row)[:, None]
    focus = pick(jnp.broadcast_to(defocus[:, None], blk_plane.shape))
    side_f = jnp.broadcast_to(side, (own, n_dev, 2, 2)).reshape(-1)
    valid = valid.reshape(-1)
    lane = lax.iota(jnp.int32, LANES)
    column_x = cols[:, None] * LANES + lane[None, :]
    fold_x = jnp.minimum(column_x, box - column_x).astype(jnp.float32)
    fold_y = jnp.minimum(rows, box - rows).astype(jnp.float32)
    wave_sq = (fold_x * fold_x + (fold_y * fold_y)[:, None]) / float(box * box)
    ctf_value = -jnp.sin(CTF_SCALE * focus[:, None] * wave_sq + CTF_PHASE)
    weight = jnp.where(side_f == 0, 1.0 - frac_z, frac_z)
    weight = jnp.where(valid, weight, 0.0)
    scale = weight[:, None] * ctf_value
    step = int(math.isqrt(n_rows))
    a = lax.iota(jnp.int32, n_rows // step)[None, :]
    b = lax.iota(jnp.int32, step)[None, :]

    def row_roots(r):
        a_re, a_im = roots(r[:, None], a * step, n_rows, 1.0)
        b_re, b_im = roots(r[:, None], b, n_rows, 1.0)
        w_re = a_re[:, :, None] * b_re[:, None, :] - a_im[:, :, None] * b_im[:, None, :]
        w_im = a_re[:, :, None] * b_im[:, None, :] + a_im[:, :, None] * b_re[:, None, :]
        return w_re.reshape(-1, n_rows), w_im.reshape(-1, n_rows)

    lo_re, lo_im = row_roots(rows)
    hi_re, hi_im = row_roots(rows + 1)
    norm = 1.0 / math.sqrt(n_rows)
    w_re = ((1.0 - frac_y) * lo_re + frac_y * hi_re) * norm
    w_im = ((1.0 - frac_y) * lo_im + frac_y * hi_im) * norm
    n_s = w_re.shape[0] // own
    w_all = jnp.stack([w_re.reshape(own, n_s, n_rows), w_im.reshape(own, n_s, n_rows)], axis=1)
    m = x // SPLIT
    step_n2 = m // len(planes)
    idx = lax.iota(jnp.int32, m)
    c_re, c_im = roots(idx[:, None], idx[None, :], m, 1.0 / math.sqrt(x))
    w_col = jnp.stack(
        [jnp.stack([c_re, -c_im], axis=1), jnp.stack([c_im, c_re], axis=1)], axis=0
    )
    y = None
    for j, piece in enumerate(planes):
        r_t = jnp.einsum("trc,tpsr->tpcs", piece, w_all, precision=MID)
        r_t = with_layout_constraint(r_t, Layout(major_to_minor=(0, 1, 2, 3)))
        r5 = r_t.reshape(own, 2, step_n2, SPLIT, n_s)
        w_j = w_col[:, :, :, j * step_n2:(j + 1) * step_n2]
        y_j = jnp.einsum("qkpn,tpnjs->tqkjs", w_j, r5, precision=MID)
        y = y_j if y is None else y + y_j
    y_re = y[:, 0]
    y_im = y[:, 1]
    n1 = lax.iota(jnp.int32, SPLIT)
    cols_t = cols.reshape(own, n_s)
    e_re, e_im = roots(n1[None, :, None], cols_t[:, None, :], SPLIT, 1.0)
    t_re, t_im = roots(lane[:, None], n1[None, :], box, 1.0)
    e_re = e_re[:, None]
    e_im = e_im[:, None]
    t_re = t_re[None, :, :, None]
    t_im = t_im[None, :, :, None]
    g_re = e_re * t_re - e_im * t_im
    g_im = e_re * t_im + e_im * t_re
    o_re = jnp.sum(g_re * y_re - g_im * y_im, axis=2)
    o_im = jnp.sum(g_re * y_im + g_im * y_re, axis=2)
    o_re = jnp.swapaxes(o_re, 1, 2).reshape(own * n_s, LANES)
    o_im = jnp.swapaxes(o_im, 1, 2).reshape(own * n_s, LANES)
    parts = jnp.stack([scale * o_re, scale * o_im], axis=1)
    parts = parts.reshape(own, n_dev, 4, 2, LANES)
    return jnp.swapaxes(parts, 0, 1).reshape(n_dev, own * 4 * 2, LANES)


def gather_parts(recv, blk_plane, me, own, n_slab, n_img):
    n_dev = n_slab * n_img
    plane, rank = slot_tables(blk_plane, n_dev)
    mine = plane[me]
    my_rank = rank[me]
    slots = own * 4

    def place(q, side):
        holder = q // own
        src = (holder % n_slab) * n_img + holder // n_slab
        return src * slots + (q % own) * 4 + side * 2 + my_rank

    flat = recv.reshape(-1, 2, LANES)
    rows = lax.iota(jnp.int32, flat.shape[0])[None, :]
    pick = (rows == place(mine, 0)[:, None]).astype(jnp.float32) + (
        rows == place(mine + 1, 1)[:, None]
    ).astype(jnp.float32)
    return jnp.einsum("kj,jpl->kpl", pick, flat, precision=MID)


def on_device(volume, blk_plane, blk_row, blk_col, frac_plane, frac_row, defocus):
    box = volume.shape[2]
    n_slab = lax.axis_size("slab")
    n_img = lax.axis_size("img")
    n_dev = n_slab * n_img
    planes = [lax.all_to_all(volume, "slab", split_axis=0, concat_axis=1, tiled=True)]
    own = planes[0].shape[0]
    first_plane = (lax.axis_index("img") * n_slab + lax.axis_index("slab")) * own
    meta = (blk_plane, blk_row, blk_col, frac_plane, frac_row, defocus)
    parts = send_parts(planes, first_plane, meta, box, n_dev)
    recv = lax.all_to_all(parts, ("slab", "img"), split_axis=0, concat_axis=0, tiled=True)
    me = lax.axis_index("slab") * n_img + lax.axis_index("img")
    total = gather_parts(recv, blk_plane, me, own, n_slab, n_img)
    n_blk = blk_plane.shape[1]
    return total.reshape(-1, n_blk, 2, LANES)


def solution(mesh):
    placed = (P("img", "slab", None), P(), P(), P(), P(), P(), P())
    return jax.shard_map(
        on_device,
        mesh=mesh,
        in_specs=placed,
        out_specs=P(("slab", "img"), None, None, None),
        check_vma=False,
    )
```

```python
import math

import jax
import jax.numpy as jnp
from jax import lax
from jax.sharding import PartitionSpec as P
from jax.experimental.layout import Layout, with_layout_constraint

LANES = 128
SPLIT = 8


CTF_SCALE = 20.0
CTF_PHASE = 0.07
MID = lax.Precision.HIGH


def roots(rows, cols, length, factor):
    phase = rows * cols % length
    angle = phase.astype(jnp.float32) * (2.0 * math.pi / length)
    return (jnp.cos(angle) * factor, -jnp.sin(angle) * factor)


def slot_tables(blk_plane, n_dev):
    plane = blk_plane.reshape(n_dev, -1)
    k_dev = plane.shape[1]
    order = lax.iota(jnp.int32, k_dev)
    same = plane[:, :, None] == plane[:, None, :]
    earlier = order[None, None, :] < order[None, :, None]
    rank = jnp.sum((same & earlier).astype(jnp.int32), axis=2)
    return plane, rank


def send_parts(planes, first_plane, meta, box, n_dev):
    blk_plane, blk_row, blk_col, frac_plane, frac_row, defocus = meta
    n_blk = blk_plane.shape[1]
    own, n_rows, width = planes[0].shape
    x = width * len(planes)
    plane_of, rank = slot_tables(blk_plane, n_dev)
    k_dev = plane_of.shape[1]
    t = lax.iota(jnp.int32, own)[:, None, None, None]
    side = lax.iota(jnp.int32, 2)[None, None, :, None]
    u = lax.iota(jnp.int32, 2)[None, None, None, :]
    target = first_plane + t - side
    match = (plane_of[None, :, None, None, :] == target[..., None]) & (
        rank[None, :, None, None, :] == u[..., None]
    )
    valid = jnp.any(match, axis=-1)
    def pick(values):
        table = values.reshape(n_dev, k_dev)[None, :, None, None, :]
        return jnp.sum(jnp.where(match, table, jnp.zeros_like(table)), axis=-1).reshape(-1)

    rows = pick(blk_row)
    cols = pick(blk_col)
    frac_z = pick(frac_plane)
    frac_y = pick(frac_row)[:, None]
    focus = pick(jnp.broadcast_to(defocus[:, None], blk_plane.shape))
    side_f = jnp.broadcast_to(side, (own, n_dev, 2, 2)).reshape(-1)
    valid = valid.reshape(-1)
    lane = lax.iota(jnp.int32, LANES)
    column_x = cols[:, None] * LANES + lane[None, :]
    fold_x = jnp.minimum(column_x, box - column_x).astype(jnp.float32)
    fold_y = jnp.minimum(rows, box - rows).astype(jnp.float32)
    wave_sq = (fold_x * fold_x + (fold_y * fold_y)[:, None]) / float(box * box)
    ctf_value = -jnp.sin(CTF_SCALE * focus[:, None] * wave_sq + CTF_PHASE)
    weight = jnp.where(side_f == 0, 1.0 - frac_z, frac_z)
    weight = jnp.where(valid, weight, 0.0)
    scale = weight[:, None] * ctf_value
    step = int(math.isqrt(n_rows))
    a = lax.iota(jnp.int32, n_rows // step)[None, :]
    b = lax.iota(jnp.int32, step)[None, :]

    def row_roots(r):
        a_re, a_im = roots(r[:, None], a * step, n_rows, 1.0)
        b_re, b_im = roots(r[:, None], b, n_rows, 1.0)
        w_re = a_re[:, :, None] * b_re[:, None, :] - a_im[:, :, None] * b_im[:, None, :]
        w_im = a_re[:, :, None] * b_im[:, None, :] + a_im[:, :, None] * b_re[:, None, :]
        return w_re.reshape(-1, n_rows), w_im.reshape(-1, n_rows)

    lo_re, lo_im = row_roots(rows)
    hi_re, hi_im = row_roots(rows + 1)
    norm = 1.0 / math.sqrt(n_rows)
    w_re = ((1.0 - frac_y) * lo_re + frac_y * hi_re) * norm
    w_im = ((1.0 - frac_y) * lo_im + frac_y * hi_im) * norm
    n_s = w_re.shape[0] // own
    w_all = jnp.stack([w_re.reshape(own, n_s, n_rows), w_im.reshape(own, n_s, n_rows)], axis=1)
    m = x // SPLIT
    step_n2 = m // len(planes)
    idx = lax.iota(jnp.int32, m)
    c_re, c_im = roots(idx[:, None], idx[None, :], m, 1.0 / math.sqrt(x))
    w_col = jnp.stack(
        [jnp.stack([c_re, -c_im], axis=1), jnp.stack([c_im, c_re], axis=1)], axis=0
    )
    y = None
    for j, piece in enumerate(planes):
        r_t = jnp.einsum("trc,tpsr->tpcs", piece, w_all, precision=MID)
        r_t = with_layout_constraint(r_t, Layout(major_to_minor=(0, 1, 2, 3)))
        r5 = r_t.reshape(own, 2, step_n2, SPLIT, n_s)
        w_j = w_col[:, :, :, j * step_n2:(j + 1) * step_n2]
        y_j = jnp.einsum("qkpn,tpnjs->tqkjs", w_j, r5, precision=MID)
        y = y_j if y is None else y + y_j
    y_re = y[:, 0]
    y_im = y[:, 1]
    n1 = lax.iota(jnp.int32, SPLIT)
    cols_t = cols.reshape(own, n_s)
    e_re, e_im = roots(n1[None, :, None], cols_t[:, None, :], SPLIT, 1.0)
    t_re, t_im = roots(lane[:, None], n1[None, :], box, 1.0)
    e_re = e_re[:, None]
    e_im = e_im[:, None]
    t_re = t_re[None, :, :, None]
    t_im = t_im[None, :, :, None]
    g_re = e_re * t_re - e_im * t_im
    g_im = e_re * t_im + e_im * t_re
    scale_t = jnp.swapaxes(scale.reshape(own, n_s, LANES), 1, 2)[:, :, None, :]
    g_re = g_re * scale_t
    g_im = g_im * scale_t
    o_re = jnp.sum(g_re * y_re - g_im * y_im, axis=2)
    o_im = jnp.sum(g_re * y_im + g_im * y_re, axis=2)
    o_re = jnp.swapaxes(o_re, 1, 2).reshape(own * n_s, LANES)
    o_im = jnp.swapaxes(o_im, 1, 2).reshape(own * n_s, LANES)
    parts = jnp.stack([o_re, o_im], axis=1)
    parts = parts.reshape(own, n_dev, 4, 2, LANES)
    return jnp.swapaxes(parts, 0, 1).reshape(n_dev, own * 4 * 2, LANES)


def gather_parts(recv, blk_plane, me, own, n_slab, n_img):
    n_dev = n_slab * n_img
    plane, rank = slot_tables(blk_plane, n_dev)
    mine = plane[me]
    my_rank = rank[me]
    slots = own * 4

    def place(q, side):
        holder = q // own
        src = (holder % n_slab) * n_img + holder // n_slab
        return src * slots + (q % own) * 4 + side * 2 + my_rank

    flat = recv.reshape(-1, 2, LANES)
    rows = lax.iota(jnp.int32, flat.shape[0])[None, :]
    pick = (rows == place(mine, 0)[:, None]).astype(jnp.float32) + (
        rows == place(mine + 1, 1)[:, None]
    ).astype(jnp.float32)
    return jnp.einsum("kj,jpl->kpl", pick, flat, precision=lax.Precision.HIGHEST)


def on_device(volume, blk_plane, blk_row, blk_col, frac_plane, frac_row, defocus):
    box = volume.shape[2]
    n_slab = lax.axis_size("slab")
    n_img = lax.axis_size("img")
    n_dev = n_slab * n_img
    planes = [lax.all_to_all(volume, "slab", split_axis=0, concat_axis=1, tiled=True)]
    own = planes[0].shape[0]
    first_plane = (lax.axis_index("img") * n_slab + lax.axis_index("slab")) * own
    meta = (blk_plane, blk_row, blk_col, frac_plane, frac_row, defocus)
    parts = send_parts(planes, first_plane, meta, box, n_dev)
    recv = lax.all_to_all(parts, ("slab", "img"), split_axis=0, concat_axis=0, tiled=True)
    me = lax.axis_index("slab") * n_img + lax.axis_index("img")
    total = gather_parts(recv, blk_plane, me, own, n_slab, n_img)
    n_blk = blk_plane.shape[1]
    return total.reshape(-1, n_blk, 2, LANES)


def solution(mesh):
    placed = (P("img", "slab", None), P(), P(), P(), P(), P(), P())
    return jax.shard_map(
        on_device,
        mesh=mesh,
        in_specs=placed,
        out_specs=P(("slab", "img"), None, None, None),
        check_vma=False,
    )
```

```python
import math

import jax
import jax.numpy as jnp
from jax import lax
from jax.sharding import PartitionSpec as P
from jax.experimental.layout import Layout, with_layout_constraint

LANES = 128
SPLIT = 8


CTF_SCALE = 20.0
CTF_PHASE = 0.07
MID = lax.Precision.HIGH


def roots(rows, cols, length, factor):
    phase = rows * cols % length
    angle = phase.astype(jnp.float32) * (2.0 * math.pi / length)
    return (jnp.cos(angle) * factor, -jnp.sin(angle) * factor)


def slot_tables(blk_plane, n_dev):
    plane = blk_plane.reshape(n_dev, -1)
    k_dev = plane.shape[1]
    order = lax.iota(jnp.int32, k_dev)
    same = plane[:, :, None] == plane[:, None, :]
    earlier = order[None, None, :] < order[None, :, None]
    rank = jnp.sum((same & earlier).astype(jnp.int32), axis=2)
    return plane, rank


def send_parts(planes, first_plane, meta, box, n_dev):
    blk_plane, blk_row, blk_col, frac_plane, frac_row, defocus = meta
    n_blk = blk_plane.shape[1]
    own, n_rows, width = planes[0].shape
    x = width * len(planes)
    plane_of, rank = slot_tables(blk_plane, n_dev)
    k_dev = plane_of.shape[1]
    t = lax.iota(jnp.int32, own)[:, None, None, None]
    side = lax.iota(jnp.int32, 2)[None, None, :, None]
    u = lax.iota(jnp.int32, 2)[None, None, None, :]
    target = first_plane + t - side
    match = (plane_of[None, :, None, None, :] == target[..., None]) & (
        rank[None, :, None, None, :] == u[..., None]
    )
    valid = jnp.any(match, axis=-1)
    def pick(values):
        table = values.reshape(n_dev, k_dev)[None, :, None, None, :]
        return jnp.sum(jnp.where(match, table, jnp.zeros_like(table)), axis=-1).reshape(-1)

    rows = pick(blk_row)
    cols = pick(blk_col)
    frac_z = pick(frac_plane)
    frac_y = pick(frac_row)[:, None]
    focus = pick(jnp.broadcast_to(defocus[:, None], blk_plane.shape))
    side_f = jnp.broadcast_to(side, (own, n_dev, 2, 2)).reshape(-1)
    valid = valid.reshape(-1)
    lane = lax.iota(jnp.int32, LANES)
    column_x = cols[:, None] * LANES + lane[None, :]
    fold_x = jnp.minimum(column_x, box - column_x).astype(jnp.float32)
    fold_y = jnp.minimum(rows, box - rows).astype(jnp.float32)
    wave_sq = (fold_x * fold_x + (fold_y * fold_y)[:, None]) / float(box * box)
    ctf_value = -jnp.sin(CTF_SCALE * focus[:, None] * wave_sq + CTF_PHASE)
    weight = jnp.where(side_f == 0, 1.0 - frac_z, frac_z)
    weight = jnp.where(valid, weight, 0.0)
    scale = weight[:, None] * ctf_value
    step = int(math.isqrt(n_rows))
    a = lax.iota(jnp.int32, n_rows // step)[None, :]
    b = lax.iota(jnp.int32, step)[None, :]

    def row_roots(r):
        a_re, a_im = roots(r[:, None], a * step, n_rows, 1.0)
        b_re, b_im = roots(r[:, None], b, n_rows, 1.0)
        w_re = a_re[:, :, None] * b_re[:, None, :] - a_im[:, :, None] * b_im[:, None, :]
        w_im = a_re[:, :, None] * b_im[:, None, :] + a_im[:, :, None] * b_re[:, None, :]
        return w_re.reshape(-1, n_rows), w_im.reshape(-1, n_rows)

    lo_re, lo_im = row_roots(rows)
    hi_re, hi_im = row_roots(rows + 1)
    norm = 1.0 / math.sqrt(n_rows)
    w_re = ((1.0 - frac_y) * lo_re + frac_y * hi_re) * norm
    w_im = ((1.0 - frac_y) * lo_im + frac_y * hi_im) * norm
    n_s = w_re.shape[0] // own
    w_all = jnp.stack([w_re.reshape(own, n_s, n_rows), w_im.reshape(own, n_s, n_rows)], axis=1)
    m = x // SPLIT
    step_n2 = m // len(planes)
    idx = lax.iota(jnp.int32, m)
    c_re, c_im = roots(idx[:, None], idx[None, :], m, 1.0 / math.sqrt(x))
    w_col = jnp.stack(
        [jnp.stack([c_re, -c_im], axis=1), jnp.stack([c_im, c_re], axis=1)], axis=0
    )
    y = None
    for j, piece in enumerate(planes):
        r_t = jnp.einsum("trc,tpsr->tpcs", piece, w_all, precision=MID)
        r_t = with_layout_constraint(r_t, Layout(major_to_minor=(0, 1, 2, 3)))
        r5 = r_t.reshape(own, 2, step_n2, SPLIT, n_s)
        w_j = w_col[:, :, :, j * step_n2:(j + 1) * step_n2]
        y_j = jnp.einsum("qkpn,tpnjs->tqkjs", w_j, r5, precision=MID)
        y = y_j if y is None else y + y_j
    y_re = y[:, 0]
    y_im = y[:, 1]
    n1 = lax.iota(jnp.int32, SPLIT)
    cols_t = cols.reshape(own, n_s)
    e_re, e_im = roots(n1[None, :, None], cols_t[:, None, :], SPLIT, 1.0)
    t_re, t_im = roots(lane[:, None], n1[None, :], box, 1.0)
    e_re = e_re[:, None]
    e_im = e_im[:, None]
    t_re = t_re[None, :, :, None]
    t_im = t_im[None, :, :, None]
    g_re = e_re * t_re - e_im * t_im
    g_im = e_re * t_im + e_im * t_re
    scale_t = jnp.swapaxes(scale.reshape(own, n_s, LANES), 1, 2)[:, :, None, :]
    g_re = g_re * scale_t
    g_im = g_im * scale_t
    o_re = jnp.sum(g_re * y_re - g_im * y_im, axis=2)
    o_im = jnp.sum(g_re * y_im + g_im * y_re, axis=2)
    o_re = jnp.swapaxes(o_re, 1, 2).reshape(own * n_s, LANES)
    o_im = jnp.swapaxes(o_im, 1, 2).reshape(own * n_s, LANES)
    p_re = jnp.swapaxes(o_re.reshape(own, n_dev, 4, LANES), 0, 1)
    p_im = jnp.swapaxes(o_im.reshape(own, n_dev, 4, LANES), 0, 1)
    return jnp.concatenate(
        [p_re.reshape(n_dev, own * 4, LANES), p_im.reshape(n_dev, own * 4, LANES)], axis=1
    )


def gather_parts(recv, blk_plane, me, own, n_slab, n_img):
    n_dev = n_slab * n_img
    plane, rank = slot_tables(blk_plane, n_dev)
    mine = plane[me]
    my_rank = rank[me]
    slots = own * 4

    def place(q, side):
        holder = q // own
        src = (holder % n_slab) * n_img + holder // n_slab
        return src * slots + (q % own) * 4 + side * 2 + my_rank

    n_src = recv.shape[0]
    split = recv.reshape(n_src, 2, slots, LANES)
    rows = lax.iota(jnp.int32, n_src * slots)[None, :]
    pick = (rows == place(mine, 0)[:, None]).astype(jnp.float32) + (
        rows == place(mine + 1, 1)[:, None]
    ).astype(jnp.float32)
    pick = pick.reshape(-1, n_src, slots)
    return jnp.einsum("kas,apsl->kpl", pick, split, precision=lax.Precision.HIGHEST)


def on_device(volume, blk_plane, blk_row, blk_col, frac_plane, frac_row, defocus):
    box = volume.shape[2]
    n_slab = lax.axis_size("slab")
    n_img = lax.axis_size("img")
    n_dev = n_slab * n_img
    planes = [lax.all_to_all(volume, "slab", split_axis=0, concat_axis=1, tiled=True)]
    own = planes[0].shape[0]
    first_plane = (lax.axis_index("img") * n_slab + lax.axis_index("slab")) * own
    meta = (blk_plane, blk_row, blk_col, frac_plane, frac_row, defocus)
    parts = send_parts(planes, first_plane, meta, box, n_dev)
    recv = lax.all_to_all(parts, ("slab", "img"), split_axis=0, concat_axis=0, tiled=True)
    me = lax.axis_index("slab") * n_img + lax.axis_index("img")
    total = gather_parts(recv, blk_plane, me, own, n_slab, n_img)
    n_blk = blk_plane.shape[1]
    return total.reshape(-1, n_blk, 2, LANES)


def solution(mesh):
    placed = (P("img", "slab", None), P(), P(), P(), P(), P(), P())
    return jax.shard_map(
        on_device,
        mesh=mesh,
        in_specs=placed,
        out_specs=P(("slab", "img"), None, None, None),
        check_vma=False,
    )
```
